32 devices in a mesh: dp: 4 (over x, core), pipe: 2 (over y), tensor: 4 (over z).
Axes of the slice: x: 2, y: 2, z: 4, core: 2. Of those that a mesh axis runs over, the one named last changes fastest.
Arguments:
- layer_input: bfloat16 [4, 2, 512, 8192], P('dp', 'pipe', None, 'tensor'), may hold values from -40 to 40
- output_grad: bfloat16 [4, 2, 512, 8192], P('dp', 'pipe', None, 'tensor'), may hold values from -6 to 6
- kv_grad: bfloat16 [4, 2, 512, 2048], P('dp', 'pipe', None, 'tensor'), may hold values from -6 to 6
- norm_gain: bfloat16 [2, 8192], P('pipe', 'tensor'), may hold values from 0.5 to 1.5
- kv_weight: bfloat16 [2, 8192, 2048], P('pipe', 'tensor'), may hold values from -0.0625 to 0.0625
Outputs:
- upstream_grad: bfloat16 [4, 2, 512, 8192], P('dp', 'pipe', None, 'tensor')
- kv_weight_grad: bfloat16 [2, 8192, 2048], P('pipe', 'tensor', 'dp')
- gain_grad: float32 [2, 8192], P('pipe', 'tensor')
The draws below stay inside these ranges and needn't reach their ends.
All inputs are finite; a program needn't handle non-finite values.
Results may differ from the reference program's by a relative error of at most 0.009.
Values may be sent and summed in bfloat16 or wider, within the bound.
No kernel may reach another device: no remote copies, remote signals or barrier semaphores. Data moves between devices by JAX's collectives and lax.ppermute only.
A program may use at most 128 MiB of HBM per device.

```python
import jax
import jax.numpy as jnp
from jax import lax

D = 8192
SEQ = 512
KV = 2048
N_DP = 4
N_PIPE = 2


def draw_layer_input(key, part):
    first, second, third = jax.random.split(key, 3)
    shape = (N_DP, N_PIPE, SEQ, D)
    position = jnp.arange(D, dtype=jnp.float32) / D
    base = jax.random.truncated_normal(first, -4.0, 4.0, shape, jnp.float32)
    trend = jnp.exp(jnp.log(3.0) * position)
    rough_col = jnp.exp(jax.random.uniform(second, (D,), jnp.float32, 0.0, jnp.log(3.3)))
    row_scale = jnp.exp(jax.random.uniform(third, (N_DP, N_PIPE, SEQ, 1), jnp.float32, 0.0, jnp.log(10.0)))
    return (0.05 * base * trend * rough_col * row_scale).astype(jnp.bfloat16)


def block_levels(own_key, dims, cuts, low, largest):
    level, own = 1.0, jax.random.fold_in(own_key, 6)
    for dim, blocks in cuts:
        steps = jnp.exp(jax.random.uniform(jax.random.fold_in(own, dim), (blocks,), jnp.float32, low / len(cuts), largest / len(cuts)))
        level = level * jnp.repeat(steps, dims[dim] // blocks).reshape([-1 if axis == dim else 1 for axis in range(len(dims))])
    return level


def gaussian(own_key, dims, spread, bound, cuts=(), kind=jnp.bfloat16):
    entries = spread * jax.random.normal(own_key, dims, jnp.float32)
    if cuts:
        entries = entries * block_levels(own_key, dims, cuts, -0.22, 0.18)
    return jnp.clip(entries, -bound, bound).astype(kind)


def setup_inputs(seed: int = 0) -> dict:
    arg_keys = jax.random.split(jax.random.key(seed), 6)
    layer_input = draw_layer_input(jax.random.fold_in(arg_keys[5], 71), 0)
    output_grad = gaussian(arg_keys[1], (N_DP, N_PIPE, SEQ, D), 1.0, 6.0, ((0, 4), (1, 2), (3, 4)))
    kv_grad = gaussian(arg_keys[2], (N_DP, N_PIPE, SEQ, KV), 1.0, 6.0, ((0, 4), (1, 2), (3, 4)))
    norm_gain = jnp.clip(1.0 + 0.1 * jax.random.normal(arg_keys[3], (N_PIPE, D), jnp.float32), 0.5, 1.5).astype(jnp.bfloat16)
    kv_weight = gaussian(arg_keys[4], (N_PIPE, D, KV), D ** -0.5, 0.0625, ((0, 2), (1, 4)))
    return dict(layer_input=layer_input, output_grad=output_grad, kv_grad=kv_grad, norm_gain=norm_gain, kv_weight=kv_weight)


def one_replica(rows, grad_out, grad_kv, gain, weight):
    values = rows.astype(jnp.float32)
    rstd = lax.rsqrt(lax.optimization_barrier(jnp.mean(values * values, axis=-1, keepdims=True)) + 1e-05)
    normed = values * rstd
    gain_f = gain.astype(jnp.float32)
    hidden = (normed * gain_f).astype(jnp.bfloat16)
    row_grad = lax.dot_general(grad_kv, weight, (((1,), (1,)), ((), ())), preferred_element_type=jnp.float32)
    scaled = gain_f * row_grad
    mean_term = lax.optimization_barrier(jnp.mean(scaled * normed, axis=-1, keepdims=True))
    input_grad = (grad_out.astype(jnp.float32) + rstd * (scaled - normed * mean_term)).astype(jnp.bfloat16)
    gain_part = lax.optimization_barrier(jnp.sum(row_grad * normed, axis=0))
    wgrad = lax.dot_general(hidden, grad_kv, (((0,), (0,)), ((), ())), preferred_element_type=jnp.float32).astype(jnp.bfloat16)
    return (input_grad, gain_part, wgrad)

def one_section(args):
    rows, grad_out, grad_kv, gain, weight = args

    def over_replicas(carry, item):
        input_grad, gain_part, wgrad = one_replica(item[0], item[1], item[2], gain, weight)
        return ((carry[0] + gain_part, carry[1] + wgrad.astype(jnp.float32)), input_grad)
    init = (jnp.zeros((D,), jnp.float32), jnp.zeros((D, KV), jnp.float32))
    (gain_total, weight_total), input_grads = lax.scan(over_replicas, init, (rows, grad_out, grad_kv))
    return (input_grads, gain_total, weight_total.astype(jnp.bfloat16))

def reference(layer_input, output_grad, kv_grad, norm_gain, kv_weight):
    stacked = (layer_input.transpose(1, 0, 2, 3), output_grad.transpose(1, 0, 2, 3), kv_grad.transpose(1, 0, 2, 3), norm_gain, kv_weight)
    input_grads, gain_grad, kv_weight_grad = lax.map(one_section, stacked)
    input_grads = input_grads.transpose(1, 0, 2, 3)
    upstream_grad = jnp.concatenate([input_grads[:, 1:], jnp.zeros_like(input_grads[:, :1])], axis=1)
    return (upstream_grad, kv_weight_grad, gain_grad)
```

```python
import jax
import jax.numpy as jnp
from jax import lax
from jax.sharding import PartitionSpec as P

EPS = 1e-05
CHUNKS = 2


def from_behind(block, axis, distance):
    devices = range(lax.axis_size(axis))
    route = [(i - distance, i) for i in devices if i - distance in devices]
    return lax.ppermute(block, axis, route)


def shifted(block, axis, shift):
    n = lax.axis_size(axis)
    return lax.ppermute(block, axis, [(i, (i + shift) % n) for i in range(n)])


def to_partner(block):
    n = lax.axis_size("dp")
    return lax.ppermute(block, "dp", [(i, i ^ 1) for i in range(n)])


def summed_over(part, axis):
    return jnp.sum(lax.all_gather(part, axis, axis=0), axis=0)


def gather_columns(block):
    n = lax.axis_size("tensor")
    me = lax.axis_index("tensor")
    rows, width = block.shape
    full = jnp.zeros((rows, width * n), block.dtype)
    full = lax.dynamic_update_slice(full, block, (0, me * width))
    for d in range(1, n):
        piece = shifted(block, "tensor", d)
        full = lax.dynamic_update_slice(full, piece, (0, ((me - d) % n) * width))
    return full


def on_device(layer_input, output_grad, kv_grad, norm_gain, kv_weight):
    rows = layer_input[0, 0]
    grad_out = output_grad[0, 0]
    grad_kv = kv_grad[0, 0]
    gain_f = norm_gain[0].astype(jnp.float32)
    weight = kv_weight[0]
    seq, d_local = rows.shape
    d_model = d_local * lax.axis_size("tensor")
    n_dp = lax.axis_size("dp")
    me = lax.axis_index("dp")
    kv = grad_kv.shape[1] * lax.axis_size("tensor")
    kv_block = kv // n_dp
    shifts = [2 * d for d in range(1, n_dp // 2)]

    rows_outer = [shifted(rows, "dp", s) for s in shifts]
    rows_partner = to_partner(rows)
    rows_partner_outer = [to_partner(r) for r in rows_outer]

    values = rows.astype(jnp.float32)
    total_squares = summed_over(jnp.sum(values * values, axis=1), "tensor")
    rstd = lax.rsqrt(total_squares / d_model + EPS)
    rstd_outer = [shifted(rstd, "dp", s) for s in shifts]
    rstd_partner = to_partner(rstd)
    rstd_partner_outer = [to_partner(r) for r in rstd_outer]
    normed = values * rstd[:, None]

    def hidden_of(x, r):
        return ((x.astype(jnp.float32) * r[:, None]) * gain_f).astype(jnp.bfloat16)

    def kv_cols(full, owner):
        return lax.dynamic_slice_in_dim(full, owner * kv_block, kv_block, axis=1)

    step = seq // CHUNKS
    inputs_grad = []
    gain_part = jnp.zeros((d_local,), jnp.float32)
    kv_own, kv_outer, kv_partner, kv_partner_outer = [], [], [], []
    for c in range(CHUNKS):
        lo = c * step
        piece = gather_columns(grad_kv[lo:lo + step])
        kv_own.append(kv_cols(piece, me))
        outer = []
        for s in shifts:
            dest = (me + s) % n_dp
            pair = jnp.concatenate([kv_cols(piece, dest), kv_cols(piece, dest ^ 1)], axis=1)
            outer.append(shifted(pair, "dp", s))
        kv_outer.append([o[:, :kv_block] for o in outer])
        kv_partner.append(to_partner(kv_cols(piece, me ^ 1)))
        kv_partner_outer.append([to_partner(o[:, kv_block:]) for o in outer])

        row_total = lax.dot_general(
            piece, weight, (((1,), (1,)), ((), ())), preferred_element_type=jnp.float32
        )
        normed_c = normed[lo:lo + step]
        scaled = gain_f * row_total
        mean_term = summed_over(jnp.sum(scaled * normed_c, axis=1), "tensor") / d_model
        input_grad = (
            grad_out[lo:lo + step].astype(jnp.float32)
            + rstd[lo:lo + step, None] * (scaled - normed_c * mean_term[:, None])
        ).astype(jnp.bfloat16)
        inputs_grad.append(from_behind(input_grad, "pipe", -1))
        gain_part = gain_part + jnp.sum(row_total * normed_c, axis=0)

    upstream = jnp.concatenate(inputs_grad, axis=0)
    gain_total = summed_over(gain_part, "dp")

    def weight_part(x, r, blocks):
        h = hidden_of(x, r)
        total = None
        for c, blk in enumerate(blocks):
            term = lax.dot_general(
                h[c * step:(c + 1) * step], blk, (((0,), (0,)), ((), ())),
                preferred_element_type=jnp.float32,
            )
            total = term if total is None else total + term
        return total

    wgrad = weight_part(rows, rstd, kv_own)
    wgrad = wgrad + weight_part(rows_partner, rstd_partner, kv_partner)
    for k in range(len(shifts)):
        wgrad = wgrad + weight_part(rows_outer[k], rstd_outer[k], [b[k] for b in kv_outer])
        wgrad = wgrad + weight_part(
            rows_partner_outer[k], rstd_partner_outer[k], [b[k] for b in kv_partner_outer]
        )
    weight_total = wgrad.astype(jnp.bfloat16)
    return (upstream[None, None], weight_total[None], gain_total[None])


def solution(mesh):
    in_specs = (
        P("dp", "pipe", None, "tensor"),
        P("dp", "pipe", None, "tensor"),
        P("dp", "pipe", None, "tensor"),
        P("pipe", "tensor"),
        P("pipe", "tensor", None),
    )
    out_specs = (P("dp", "pipe", None, "tensor"), P("pipe", "tensor", "dp"), P("pipe", "tensor"))
    return jax.shard_map(
        on_device, mesh=mesh, in_specs=in_specs, out_specs=out_specs, check_vma=False
    )
```

```python
import jax
import jax.numpy as jnp
from jax import lax
from jax.sharding import PartitionSpec as P

EPS = 1e-05
CHUNKS = 2


def from_behind(block, axis, distance):
    devices = range(lax.axis_size(axis))
    route = [(i - distance, i) for i in devices if i - distance in devices]
    return lax.ppermute(block, axis, route)


def shifted(block, axis, shift):
    n = lax.axis_size(axis)
    return lax.ppermute(block, axis, [(i, (i + shift) % n) for i in range(n)])


def to_partner(block):
    n = lax.axis_size("dp")
    return lax.ppermute(block, "dp", [(i, i ^ 1) for i in range(n)])


def gather_columns(block):
    n = lax.axis_size("tensor")
    me = lax.axis_index("tensor")
    rows, width = block.shape
    full = jnp.zeros((rows, width * n), block.dtype)
    full = lax.dynamic_update_slice(full, block, (0, me * width))
    for d in range(1, n):
        piece = shifted(block, "tensor", d)
        full = lax.dynamic_update_slice(full, piece, (0, ((me - d) % n) * width))
    return full


def on_device(layer_input, output_grad, kv_grad, norm_gain, kv_weight):
    rows = layer_input[0, 0]
    grad_out = output_grad[0, 0]
    grad_kv = kv_grad[0, 0]
    gain_f = norm_gain[0].astype(jnp.float32)
    weight = kv_weight[0]
    seq, d_local = rows.shape
    d_model = d_local * lax.axis_size("tensor")
    n_dp = lax.axis_size("dp")
    me = lax.axis_index("dp")
    kv = grad_kv.shape[1] * lax.axis_size("tensor")
    kv_block = kv // n_dp
    shifts = [2 * d for d in range(1, n_dp // 2)]

    values = rows.astype(jnp.float32)
    total_squares = lax.psum(jnp.sum(values * values, axis=1, keepdims=True), "tensor")
    rstd = lax.rsqrt(total_squares / d_model + EPS)
    normed = values * rstd
    hidden = (normed * gain_f).astype(jnp.bfloat16)

    hidden_outer = [shifted(hidden, "dp", s) for s in shifts]
    hidden_partner = to_partner(hidden)
    hidden_partner_outer = [to_partner(h) for h in hidden_outer]

    piece = gather_columns(grad_kv)

    def kv_cols(owner):
        return lax.dynamic_slice_in_dim(piece, owner * kv_block, kv_block, axis=1)

    kv_outer = []
    for s in shifts:
        dest = (me + s) % n_dp
        kv_outer.append(shifted(jnp.concatenate([kv_cols(dest), kv_cols(dest ^ 1)], axis=1), "dp", s))
    to_send = jnp.concatenate([kv_cols(me ^ 1)] + [o[:, kv_block:] for o in kv_outer], axis=1)
    kv_partner_all = to_partner(to_send)
    kv_partner = kv_partner_all[:, :kv_block]
    kv_partner_outer = [
        kv_partner_all[:, (k + 1) * kv_block:(k + 2) * kv_block] for k in range(len(shifts))
    ]

    step = seq // CHUNKS
    inputs_grad = []
    sent = []
    gain_part = jnp.zeros((d_local,), jnp.float32)
    block = piece[:step]
    for c in range(CHUNKS):
        lo = c * step
        row_total = lax.dot_general(
            block, weight, (((1,), (1,)), ((), ())),
            preferred_element_type=jnp.float32,
        )
        normed_c = normed[lo:lo + step]
        scaled = gain_f * row_total
        mean_term = lax.psum(jnp.sum(scaled * normed_c, axis=1, keepdims=True), "tensor") / d_model
        input_grad = (
            grad_out[lo:lo + step].astype(jnp.float32)
            + rstd[lo:lo + step] * (scaled - normed_c * mean_term)
        ).astype(jnp.bfloat16)
        inputs_grad.append(from_behind(input_grad, "pipe", -1))
        sent.append(input_grad)
        if c + 1 < CHUNKS:
            _, block = lax.optimization_barrier((input_grad, piece[lo + step:lo + 2 * step]))
        gain_part = gain_part + jnp.sum(row_total * normed_c, axis=0)

    upstream = jnp.concatenate(inputs_grad, axis=0)
    gain_total = lax.psum(gain_part, "dp")

    _, hidden_own = lax.optimization_barrier((sent, hidden))

    def term(h, blk):
        return lax.dot_general(h, blk, (((0,), (0,)), ((), ())), preferred_element_type=jnp.float32)

    wgrad = term(hidden_own, kv_cols(me))
    wgrad = wgrad + term(hidden_partner, kv_partner)
    for k in range(len(shifts)):
        wgrad = wgrad + term(hidden_outer[k], kv_outer[k][:, :kv_block])
        wgrad = wgrad + term(hidden_partner_outer[k], kv_partner_outer[k])
    weight_total = wgrad.astype(jnp.bfloat16)
    return (upstream[None, None], weight_total[None], gain_total[None])


def solution(mesh):
    in_specs = (
        P("dp", "pipe", None, "tensor"),
        P("dp", "pipe", None, "tensor"),
        P("dp", "pipe", None, "tensor"),
        P("pipe", "tensor"),
        P("pipe", "tensor", None),
    )
    out_specs = (P("dp", "pipe", None, "tensor"), P("pipe", "tensor", "dp"), P("pipe", "tensor"))
    return jax.shard_map(
        on_device, mesh=mesh, in_specs=in_specs, out_specs=out_specs, check_vma=False
    )
```

```python
import jax
import jax.numpy as jnp
from jax import lax
from jax.sharding import PartitionSpec as P

EPS = 1e-05
CHUNKS = 2


def from_behind(block, axis, distance):
    devices = range(lax.axis_size(axis))
    route = [(i - distance, i) for i in devices if i - distance in devices]
    return lax.ppermute(block, axis, route)


def shifted(block, axis, shift):
    n = lax.axis_size(axis)
    return lax.ppermute(block, axis, [(i, (i + shift) % n) for i in range(n)])


def to_partner(block):
    n = lax.axis_size("dp")
    return lax.ppermute(block, "dp", [(i, i ^ 1) for i in range(n)])


def place(parts, axis):
    n = lax.axis_size(axis)
    me = lax.axis_index(axis)
    out = jnp.zeros((n,) + parts[0].shape, parts[0].dtype)
    for d, p in enumerate(parts):
        out = lax.dynamic_update_slice_in_dim(out, p[None], (me - d) % n, axis=0)
    return out


def summed(part, axis):
    n = lax.axis_size(axis)
    parts = [part] + [shifted(part, axis, d) for d in range(1, n)]
    return jnp.sum(place(parts, axis), axis=0)


def on_device(layer_input, output_grad, kv_grad, norm_gain, kv_weight):
    rows = layer_input[0, 0]
    grad_out = output_grad[0, 0]
    grad_kv = kv_grad[0, 0]
    gain_f = norm_gain[0].astype(jnp.float32)
    weight = kv_weight[0]
    seq, d_local = rows.shape
    n_t = lax.axis_size("tensor")
    d_model = d_local * n_t
    n_dp = lax.axis_size("dp")
    me = lax.axis_index("dp")
    width = grad_kv.shape[1]
    kv_block = width * n_t // n_dp
    shifts = [2 * d for d in range(1, n_dp // 2)]

    rows_outer = [shifted(rows, "dp", s) for s in shifts]
    rows_partner = to_partner(rows)
    rows_partner_outer = [to_partner(r) for r in rows_outer]

    values = rows.astype(jnp.float32)
    squares = jnp.sum(values * values, axis=1)

    t_me = lax.axis_index("tensor")
    piece = jnp.zeros((seq, width * n_t), grad_kv.dtype)
    piece = lax.dynamic_update_slice(piece, grad_kv, (0, t_me * width))
    square_parts = [squares]
    for d in range(1, n_t):
        blk, sq = shifted((grad_kv, squares), "tensor", d)
        piece = lax.dynamic_update_slice(piece, blk, (0, ((t_me - d) % n_t) * width))
        square_parts.append(sq)
    total_squares = jnp.sum(place(square_parts, "tensor"), axis=0)
    rstd = lax.rsqrt(total_squares / d_model + EPS)[:, None]
    normed = values * rstd

    def kv_cols(owner):
        return lax.dynamic_slice_in_dim(piece, owner * kv_block, kv_block, axis=1)

    kv_outer, rstd_outer = [], []
    for s in shifts:
        dest = (me + s) % n_dp
        pair = jnp.concatenate([kv_cols(dest), kv_cols(dest ^ 1)], axis=1)
        got_kv, got_rstd = shifted((pair, rstd), "dp", s)
        kv_outer.append(got_kv)
        rstd_outer.append(got_rstd)
    send_kv = jnp.concatenate([kv_cols(me ^ 1)] + [o[:, kv_block:] for o in kv_outer], axis=1)
    send_rstd = jnp.concatenate([rstd] + rstd_outer, axis=1)
    kv_partner_all, rstd_partner_all = to_partner((send_kv, send_rstd))

    step = seq // CHUNKS
    inputs_grad = []
    sent = []
    gain_part = jnp.zeros((d_local,), jnp.float32)
    block = piece[:step]
    for c in range(CHUNKS):
        lo = c * step
        row_total = lax.dot_general(
            block, weight, (((1,), (1,)), ((), ())), preferred_element_type=jnp.float32
        )
        normed_c = normed[lo:lo + step]
        scaled = gain_f * row_total
        mean_term = summed(jnp.sum(scaled * normed_c, axis=1), "tensor")[:, None] / d_model
        input_grad = (
            grad_out[lo:lo + step].astype(jnp.float32)
            + rstd[lo:lo + step] * (scaled - normed_c * mean_term)
        ).astype(jnp.bfloat16)
        inputs_grad.append(from_behind(input_grad, "pipe", -1))
        sent.append(input_grad)
        gain_part = gain_part + jnp.sum(row_total * normed_c, axis=0)
        if c + 1 < CHUNKS:
            _, block = lax.optimization_barrier((input_grad, piece[lo + step:lo + 2 * step]))

    upstream = jnp.concatenate(inputs_grad, axis=0)
    gain_total = summed(gain_part, "dp")

    _, rows_own = lax.optimization_barrier((sent, rows))

    def term(x, r, blk):
        h = ((x.astype(jnp.float32) * r) * gain_f).astype(jnp.bfloat16)
        return lax.dot_general(h, blk, (((0,), (0,)), ((), ())), preferred_element_type=jnp.float32)

    wgrad = term(rows_own, rstd, kv_cols(me))
    wgrad = wgrad + term(rows_partner, rstd_partner_all[:, :1], kv_partner_all[:, :kv_block])
    for k in range(len(shifts)):
        wgrad = wgrad + term(rows_outer[k], rstd_outer[k], kv_outer[k][:, :kv_block])
        wgrad = wgrad + term(
            rows_partner_outer[k],
            rstd_partner_all[:, k + 1:k + 2],
            kv_partner_all[:, (k + 1) * kv_block:(k + 2) * kv_block],
        )
    weight_total = wgrad.astype(jnp.bfloat16)
    return (upstream[None, None], weight_total[None], gain_total[None])


def solution(mesh):
    in_specs = (
        P("dp", "pipe", None, "tensor"),
        P("dp", "pipe", None, "tensor"),
        P("dp", "pipe", None, "tensor"),
        P("pipe", "tensor"),
        P("pipe", "tensor", None),
    )
    out_specs = (P("dp", "pipe", None, "tensor"), P("pipe", "tensor", "dp"), P("pipe", "tensor"))
    return jax.shard_map(
        on_device, mesh=mesh, in_specs=in_specs, out_specs=out_specs, check_vma=False
    )
```

```python
import jax
import jax.numpy as jnp
from jax import lax
from jax.sharding import PartitionSpec as P

EPS = 1e-05
CHUNKS = 2


def from_behind(block, axis, distance):
    devices = range(lax.axis_size(axis))
    route = [(i - distance, i) for i in devices if i - distance in devices]
    return lax.ppermute(block, axis, route)


def shifted(block, axis, shift):
    n = lax.axis_size(axis)
    return lax.ppermute(block, axis, [(i, (i + shift) % n) for i in range(n)])


def to_partner(block):
    n = lax.axis_size("dp")
    return lax.ppermute(block, "dp", [(i, i ^ 1) for i in range(n)])


def on_device(layer_input, output_grad, kv_grad, norm_gain, kv_weight):
    rows = layer_input[0, 0]
    grad_out = output_grad[0, 0]
    grad_kv = kv_grad[0, 0]
    gain_f = norm_gain[0].astype(jnp.float32)
    weight = kv_weight[0]
    seq, d_local = rows.shape
    d_model = d_local * lax.axis_size("tensor")
    n_dp = lax.axis_size("dp")
    me = lax.axis_index("dp")
    parity = me % 2
    kv_block = grad_kv.shape[1] * lax.axis_size("tensor") // n_dp
    groups = n_dp // 2

    values = rows.astype(jnp.float32)
    total_squares = lax.psum(jnp.sum(values * values, axis=1, keepdims=True), "tensor")
    rstd = lax.rsqrt(total_squares / d_model + EPS)
    normed = values * rstd
    hidden = (normed * gain_f).astype(jnp.bfloat16)
    hidden_partner = to_partner(hidden)

    piece = lax.all_gather(grad_kv, "tensor", axis=1, tiled=True)

    def cols_of(p):
        return jnp.concatenate(
            [lax.dynamic_slice_in_dim(piece, (2 * g + p) * kv_block, kv_block, axis=1) for g in range(groups)],
            axis=1,
        )

    cols_partner = to_partner(cols_of(1 - parity))
    cols_own = cols_of(parity)

    step = seq // CHUNKS
    inputs_grad = []
    gain_part = jnp.zeros((d_local,), jnp.float32)
    block = piece[:step]
    weight_total = None
    for c in range(CHUNKS):
        lo = c * step
        row_total = lax.dot_general(
            block, weight, (((1,), (1,)), ((), ())), preferred_element_type=jnp.float32
        )
        normed_c = normed[lo:lo + step]
        scaled = gain_f * row_total
        mean_term = lax.psum(jnp.sum(scaled * normed_c, axis=1, keepdims=True), "tensor") / d_model
        input_grad = (
            grad_out[lo:lo + step].astype(jnp.float32)
            + rstd[lo:lo + step] * (scaled - normed_c * mean_term)
        ).astype(jnp.bfloat16)
        inputs_grad.append(from_behind(input_grad, "pipe", -1))
        gain_part = gain_part + jnp.sum(row_total * normed_c, axis=0)
        if c == 0:
            _, h_own = lax.optimization_barrier((input_grad, hidden))
            pair = lax.dot_general(
                h_own, cols_own, (((0,), (0,)), ((), ())), preferred_element_type=jnp.float32
            ) + lax.dot_general(
                hidden_partner, cols_partner, (((0,), (0,)), ((), ())),
                preferred_element_type=jnp.float32,
            )
            own_g = me // 2
            total = lax.dynamic_slice_in_dim(pair, own_g * kv_block, kv_block, axis=1)
            for d in range(1, groups):
                dest_g = (own_g + d) % groups
                out = lax.dynamic_slice_in_dim(pair, dest_g * kv_block, kv_block, axis=1)
                total = total + shifted(out.astype(jnp.bfloat16), "dp", 2 * d).astype(jnp.float32)
            weight_total = total.astype(jnp.bfloat16)
        if c + 1 < CHUNKS:
            _, block = lax.optimization_barrier((pair, piece[lo + step:lo + 2 * step]))

    upstream = jnp.concatenate(inputs_grad, axis=0)
    gain_total = lax.psum(gain_part, "dp")
    return (upstream[None, None], weight_total[None], gain_total[None])


def solution(mesh):
    in_specs = (
        P("dp", "pipe", None, "tensor"),
        P("dp", "pipe", None, "tensor"),
        P("dp", "pipe", None, "tensor"),
        P("pipe", "tensor"),
        P("pipe", "tensor", None),
    )
    out_specs = (P("dp", "pipe", None, "tensor"), P("pipe", "tensor", "dp"), P("pipe", "tensor"))
    return jax.shard_map(
        on_device, mesh=mesh, in_specs=in_specs, out_specs=out_specs, check_vma=False
    )
```

```python
import jax
import jax.numpy as jnp
from jax import lax
from jax.sharding import PartitionSpec as P

EPS = 1e-05
CHUNKS = 2


def from_behind(block, axis, distance):
    devices = range(lax.axis_size(axis))
    route = [(i - distance, i) for i in devices if i - distance in devices]
    return lax.ppermute(block, axis, route)


def shifted(block, axis, shift):
    n = lax.axis_size(axis)
    return lax.ppermute(block, axis, [(i, (i + shift) % n) for i in range(n)])


def to_partner(block):
    n = lax.axis_size("dp")
    return lax.ppermute(block, "dp", [(i, i ^ 1) for i in range(n)])


def on_device(layer_input, output_grad, kv_grad, norm_gain, kv_weight):
    rows = layer_input[0, 0]
    grad_out = output_grad[0, 0]
    grad_kv = kv_grad[0, 0]
    gain_f = norm_gain[0].astype(jnp.float32)
    weight = kv_weight[0]
    seq, d_local = rows.shape
    d_model = d_local * lax.axis_size("tensor")
    n_dp = lax.axis_size("dp")
    me = lax.axis_index("dp")
    parity = me % 2
    kv_block = grad_kv.shape[1] * lax.axis_size("tensor") // n_dp
    groups = n_dp // 2

    values = rows.astype(jnp.float32)
    total_squares = lax.psum(jnp.sum(values * values, axis=1, keepdims=True), "tensor")
    rstd = lax.rsqrt(total_squares / d_model + EPS)
    normed = values * rstd
    hidden = (normed * gain_f).astype(jnp.bfloat16)
    hidden_partner = to_partner(hidden)

    piece = lax.all_gather(grad_kv, "tensor", axis=1, tiled=True)

    def cols_of(p):
        return jnp.concatenate(
            [lax.dynamic_slice_in_dim(piece, (2 * g + p) * kv_block, kv_block, axis=1) for g in range(groups)],
            axis=1,
        )

    cols_partner = to_partner(cols_of(1 - parity))
    cols_own = cols_of(parity)

    step = seq // CHUNKS

    def row_sums(part):
        wide = jnp.broadcast_to(part[:, None], (part.shape[0], 128))
        return lax.psum(wide, "tensor")[:, :1]

    rows_total, means = [], []
    block = piece[:step]
    for c in range(CHUNKS):
        lo = c * step
        row_total = lax.dot_general(
            block, weight, (((1,), (1,)), ((), ())), preferred_element_type=jnp.float32
        )
        scaled = gain_f * row_total
        means.append(row_sums(jnp.sum(scaled * normed[lo:lo + step], axis=1)) / d_model)
        rows_total.append(row_total)
        if c + 1 < CHUNKS:
            _, block = lax.optimization_barrier((row_total, piece[lo + step:lo + 2 * step]))

    inputs_grad = []
    gain_part = jnp.zeros((d_local,), jnp.float32)
    weight_total = None
    for c in range(CHUNKS):
        lo = c * step
        row_total = rows_total[c]
        normed_c = normed[lo:lo + step]
        scaled = gain_f * row_total
        input_grad = (
            grad_out[lo:lo + step].astype(jnp.float32)
            + rstd[lo:lo + step] * (scaled - normed_c * means[c])
        ).astype(jnp.bfloat16)
        inputs_grad.append(from_behind(input_grad, "pipe", -1))
        gain_part = gain_part + jnp.sum(row_total * normed_c, axis=0)
        if c == 0:
            _, h_own = lax.optimization_barrier((input_grad, hidden))
            pair = lax.dot_general(
                h_own, cols_own, (((0,), (0,)), ((), ())), preferred_element_type=jnp.float32
            ) + lax.dot_general(
                hidden_partner, cols_partner, (((0,), (0,)), ((), ())),
                preferred_element_type=jnp.float32,
            )
            own_g = me // 2
            total = lax.dynamic_slice_in_dim(pair, own_g * kv_block, kv_block, axis=1)
            outs = []
            for d in range(1, groups):
                dest_g = (own_g + d) % groups
                out = lax.dynamic_slice_in_dim(pair, dest_g * kv_block, kv_block, axis=1)
                outs.append(out.astype(jnp.bfloat16))
            for d, out in enumerate(outs, start=1):
                total = total + shifted(out, "dp", 2 * d).astype(jnp.float32)
            weight_total = total.astype(jnp.bfloat16)
            if c + 1 < CHUNKS:
                _, rows_total = lax.optimization_barrier((outs, rows_total))

    upstream = jnp.concatenate(inputs_grad, axis=0)
    gain_total = lax.psum(jnp.broadcast_to(gain_part[None], (8, d_local)), "dp")[0]
    return (upstream[None, None], weight_total[None], gain_total[None])


def solution(mesh):
    in_specs = (
        P("dp", "pipe", None, "tensor"),
        P("dp", "pipe", None, "tensor"),
        P("dp", "pipe", None, "tensor"),
        P("pipe", "tensor"),
        P("pipe", "tensor", None),
    )
    out_specs = (P("dp", "pipe", None, "tensor"), P("pipe", "tensor", "dp"), P("pipe", "tensor"))
    return jax.shard_map(
        on_device, mesh=mesh, in_specs=in_specs, out_specs=out_specs, check_vma=False
    )
```

```python
import jax
import jax.numpy as jnp
from jax import lax
from jax.sharding import PartitionSpec as P

EPS = 1e-05
CHUNKS = 2


def from_behind(block, axis, distance):
    devices = range(lax.axis_size(axis))
    route = [(i - distance, i) for i in devices if i - distance in devices]
    return lax.ppermute(block, axis, route)


def shifted(block, axis, shift):
    n = lax.axis_size(axis)
    return lax.ppermute(block, axis, [(i, (i + shift) % n) for i in range(n)])


def to_partner(block):
    n = lax.axis_size("dp")
    return lax.ppermute(block, "dp", [(i, i ^ 1) for i in range(n)])


def on_device(layer_input, output_grad, kv_grad, norm_gain, kv_weight):
    rows = layer_input[0, 0]
    grad_out = output_grad[0, 0]
    grad_kv = kv_grad[0, 0]
    gain_f = norm_gain[0].astype(jnp.float32)
    weight = kv_weight[0]
    seq, d_local = rows.shape
    d_model = d_local * lax.axis_size("tensor")
    n_dp = lax.axis_size("dp")
    me = lax.axis_index("dp")
    parity = me % 2
    kv_block = grad_kv.shape[1] * lax.axis_size("tensor") // n_dp
    groups = n_dp // 2

    values = rows.astype(jnp.float32)
    total_squares = lax.psum(jnp.sum(values * values, axis=1, keepdims=True), "tensor")
    rstd = lax.rsqrt(total_squares / d_model + EPS)
    normed = values * rstd
    hidden = (normed * gain_f).astype(jnp.bfloat16)
    hidden_partner = to_partner(hidden)

    piece = lax.all_gather(grad_kv, "tensor", axis=1, tiled=True)

    def cols_of(p):
        return jnp.concatenate(
            [lax.dynamic_slice_in_dim(piece, (2 * g + p) * kv_block, kv_block, axis=1) for g in range(groups)],
            axis=1,
        )

    cols_partner = to_partner(cols_of(1 - parity))
    cols_own = cols_of(parity)

    step = seq // CHUNKS
    inputs_grad = []
    gain_part = jnp.zeros((d_local,), jnp.float32)
    block = piece[:step]
    weight_total = None
    for c in range(CHUNKS):
        lo = c * step
        row_total = lax.dot_general(
            block, weight, (((1,), (1,)), ((), ())), preferred_element_type=jnp.float32
        )
        normed_c = normed[lo:lo + step]
        scaled = gain_f * row_total
        mean_term = lax.psum(jnp.sum(scaled * normed_c, axis=1, keepdims=True), "tensor") / d_model
        input_grad = (
            grad_out[lo:lo + step].astype(jnp.float32)
            + rstd[lo:lo + step] * (scaled - normed_c * mean_term)
        ).astype(jnp.bfloat16)
        inputs_grad.append(from_behind(input_grad, "pipe", -1))
        gain_part = gain_part + jnp.sum(row_total * normed_c, axis=0)
        if c == 0:
            _, h_own = lax.optimization_barrier((input_grad, hidden))
            pair = lax.dot_general(
                h_own, cols_own, (((0,), (0,)), ((), ())), preferred_element_type=jnp.float32
            ) + lax.dot_general(
                hidden_partner, cols_partner, (((0,), (0,)), ((), ())),
                preferred_element_type=jnp.float32,
            )
            own_g = me // 2
            total = lax.dynamic_slice_in_dim(pair, own_g * kv_block, kv_block, axis=1)
            outs = []
            for d in range(1, groups):
                dest_g = (own_g + d) % groups
                out = lax.dynamic_slice_in_dim(pair, dest_g * kv_block, kv_block, axis=1)
                outs.append(out.astype(jnp.bfloat16))
            for d, out in enumerate(outs, start=1):
                total = total + shifted(out, "dp", 2 * d).astype(jnp.float32)
            weight_total = total.astype(jnp.bfloat16)
        if c + 1 < CHUNKS:
            _, block = lax.optimization_barrier(((input_grad, outs), piece[lo + step:lo + 2 * step]))

    upstream = jnp.concatenate(inputs_grad, axis=0)
    pair_gain = gain_part + to_partner(gain_part)
    own_g = me // 2
    stacked = jnp.zeros((groups, d_local), jnp.float32)
    stacked = lax.dynamic_update_slice_in_dim(stacked, pair_gain[None], own_g, axis=0)
    for d in range(1, groups):
        got = shifted(pair_gain, "dp", 2 * d)
        stacked = lax.dynamic_update_slice_in_dim(stacked, got[None], (own_g - d) % groups, axis=0)
    gain_total = jnp.sum(stacked, axis=0)
    return (upstream[None, None], weight_total[None], gain_total[None])


def solution(mesh):
    in_specs = (
        P("dp", "pipe", None, "tensor"),
        P("dp", "pipe", None, "tensor"),
        P("dp", "pipe", None, "tensor"),
        P("pipe", "tensor"),
        P("pipe", "tensor", None),
    )
    out_specs = (P("dp", "pipe", None, "tensor"), P("pipe", "tensor", "dp"), P("pipe", "tensor"))
    return jax.shard_map(
        on_device, mesh=mesh, in_specs=in_specs, out_specs=out_specs, check_vma=False
    )
```

```python
import jax
import jax.numpy as jnp
from jax import lax
from jax.sharding import PartitionSpec as P

EPS = 1e-05
CHUNKS = 2


def from_behind(block, axis, distance):
    devices = range(lax.axis_size(axis))
    route = [(i - distance, i) for i in devices if i - distance in devices]
    return lax.ppermute(block, axis, route)


def shifted(block, axis, shift):
    n = lax.axis_size(axis)
    return lax.ppermute(block, axis, [(i, (i + shift) % n) for i in range(n)])


def to_partner(block):
    n = lax.axis_size("dp")
    return lax.ppermute(block, "dp", [(i, i ^ 1) for i in range(n)])


def on_device(layer_input, output_grad, kv_grad, norm_gain, kv_weight):
    rows = layer_input[0, 0]
    grad_out = output_grad[0, 0]
    grad_kv = kv_grad[0, 0]
    gain_f = norm_gain[0].astype(jnp.float32)
    weight = kv_weight[0]
    seq, d_local = rows.shape
    d_model = d_local * lax.axis_size("tensor")
    n_dp = lax.axis_size("dp")
    me = lax.axis_index("dp")
    parity = me % 2
    kv_block = grad_kv.shape[1] * lax.axis_size("tensor") // n_dp
    groups = n_dp // 2

    values = rows.astype(jnp.float32)
    total_squares = lax.psum(jnp.sum(values * values, axis=1, keepdims=True), "tensor")
    rstd = lax.rsqrt(total_squares / d_model + EPS)
    normed = values * rstd
    hidden = (normed * gain_f).astype(jnp.bfloat16)
    hidden_partner = to_partner(hidden)

    step = seq // CHUNKS
    pieces = [
        lax.all_gather(grad_kv[c * step:(c + 1) * step], "tensor", axis=1, tiled=True)
        for c in range(CHUNKS)
    ]
    piece = jnp.concatenate(pieces, axis=0)

    def cols_of(p):
        return jnp.concatenate(
            [lax.dynamic_slice_in_dim(piece, (2 * g + p) * kv_block, kv_block, axis=1) for g in range(groups)],
            axis=1,
        )


    inputs_grad = []
    gain_part = jnp.zeros((d_local,), jnp.float32)
    block = pieces[0]
    weight_total = None
    for c in range(CHUNKS):
        lo = c * step
        row_total = lax.dot_general(
            block, weight, (((1,), (1,)), ((), ())), preferred_element_type=jnp.float32
        )
        normed_c = normed[lo:lo + step]
        scaled = gain_f * row_total
        mean_term = lax.psum(jnp.sum(scaled * normed_c, axis=1, keepdims=True), "tensor") / d_model
        input_grad = (
            grad_out[lo:lo + step].astype(jnp.float32)
            + rstd[lo:lo + step] * (scaled - normed_c * mean_term)
        ).astype(jnp.bfloat16)
        inputs_grad.append(from_behind(input_grad, "pipe", -1))
        gain_part = gain_part + jnp.sum(row_total * normed_c, axis=0)
        if c == 0:
            _, (h_own, piece) = lax.optimization_barrier((input_grad, (hidden, piece)))
            cols_partner = to_partner(cols_of(1 - parity))
            cols_own = cols_of(parity)
            pair = lax.dot_general(
                h_own, cols_own, (((0,), (0,)), ((), ())), preferred_element_type=jnp.float32
            ) + lax.dot_general(
                hidden_partner, cols_partner, (((0,), (0,)), ((), ())),
                preferred_element_type=jnp.float32,
            )
            own_g = me // 2
            total = lax.dynamic_slice_in_dim(pair, own_g * kv_block, kv_block, axis=1)
            outs = []
            for d in range(1, groups):
                dest_g = (own_g + d) % groups
                out = lax.dynamic_slice_in_dim(pair, dest_g * kv_block, kv_block, axis=1)
                outs.append(out.astype(jnp.bfloat16))
            for d, out in enumerate(outs, start=1):
                total = total + shifted(out, "dp", 2 * d).astype(jnp.float32)
            weight_total = total.astype(jnp.bfloat16)
        if c + 1 < CHUNKS:
            _, block = lax.optimization_barrier(((input_grad, outs), pieces[c + 1]))

    upstream = jnp.concatenate(inputs_grad, axis=0)
    pair_gain = gain_part + to_partner(gain_part)
    own_g = me // 2
    stacked = jnp.zeros((groups, d_local), jnp.float32)
    stacked = lax.dynamic_update_slice_in_dim(stacked, pair_gain[None], own_g, axis=0)
    for d in range(1, groups):
        got = shifted(pair_gain, "dp", 2 * d)
        stacked = lax.dynamic_update_slice_in_dim(stacked, got[None], (own_g - d) % groups, axis=0)
    gain_total = jnp.sum(stacked, axis=0)
    return (upstream[None, None], weight_total[None], gain_total[None])


def solution(mesh):
    in_specs = (
        P("dp", "pipe", None, "tensor"),
        P("dp", "pipe", None, "tensor"),
        P("dp", "pipe", None, "tensor"),
        P("pipe", "tensor"),
        P("pipe", "tensor", None),
    )
    out_specs = (P("dp", "pipe", None, "tensor"), P("pipe", "tensor", "dp"), P("pipe", "tensor"))
    return jax.shard_map(
        on_device, mesh=mesh, in_specs=in_specs, out_specs=out_specs, check_vma=False
    )
```

```python
import jax
import jax.numpy as jnp
from jax import lax
from jax.sharding import PartitionSpec as P

EPS = 1e-05
CHUNKS = 2


def from_behind(block, axis, distance):
    devices = range(lax.axis_size(axis))
    route = [(i - distance, i) for i in devices if i - distance in devices]
    return lax.ppermute(block, axis, route)


def shifted(block, axis, shift):
    n = lax.axis_size(axis)
    return lax.ppermute(block, axis, [(i, (i + shift) % n) for i in range(n)])


def to_partner(block):
    n = lax.axis_size("dp")
    return lax.ppermute(block, "dp", [(i, i ^ 1) for i in range(n)])


def gather_columns(block):
    n = lax.axis_size("tensor")
    me = lax.axis_index("tensor")
    rows, width = block.shape
    full = jnp.zeros((rows, width * n), block.dtype)
    full = lax.dynamic_update_slice(full, block, (0, me * width))
    for d in range(1, n):
        got = shifted(block, "tensor", d)
        full = lax.dynamic_update_slice(full, got, (0, ((me - d) % n) * width))
    return full


def on_device(layer_input, output_grad, kv_grad, norm_gain, kv_weight):
    rows = layer_input[0, 0]
    grad_out = output_grad[0, 0]
    grad_kv = kv_grad[0, 0]
    gain_f = norm_gain[0].astype(jnp.float32)
    weight = kv_weight[0]
    seq, d_local = rows.shape
    d_model = d_local * lax.axis_size("tensor")
    n_dp = lax.axis_size("dp")
    me = lax.axis_index("dp")
    parity = me % 2
    kv_block = grad_kv.shape[1] * lax.axis_size("tensor") // n_dp
    groups = n_dp // 2

    values = rows.astype(jnp.float32)
    total_squares = lax.psum(jnp.sum(values * values, axis=1, keepdims=True), "tensor")
    rstd = lax.rsqrt(total_squares / d_model + EPS)
    normed = values * rstd
    hidden = (normed * gain_f).astype(jnp.bfloat16)
    hidden_partner = to_partner(hidden)

    step = seq // CHUNKS
    pieces = [gather_columns(grad_kv[c * step:(c + 1) * step]) for c in range(CHUNKS)]

    def cols_of(parts, p):
        return jnp.concatenate(
            [
                jnp.concatenate(
                    [lax.dynamic_slice_in_dim(q, (2 * g + p) * kv_block, kv_block, axis=1) for g in range(groups)],
                    axis=1,
                )
                for q in parts
            ],
            axis=0,
        )


    inputs_grad = []
    gain_part = jnp.zeros((d_local,), jnp.float32)
    block = pieces[0]
    weight_total = None
    for c in range(CHUNKS):
        lo = c * step
        row_total = lax.dot_general(
            block, weight, (((1,), (1,)), ((), ())), preferred_element_type=jnp.float32
        )
        normed_c = normed[lo:lo + step]
        scaled = gain_f * row_total
        mean_term = lax.psum(jnp.sum(scaled * normed_c, axis=1, keepdims=True), "tensor") / d_model
        input_grad = (
            grad_out[lo:lo + step].astype(jnp.float32)
            + rstd[lo:lo + step] * (scaled - normed_c * mean_term)
        ).astype(jnp.bfloat16)
        inputs_grad.append(from_behind(input_grad, "pipe", -1))
        gain_part = gain_part + jnp.sum(row_total * normed_c, axis=0)
        if c == 0:
            _, (h_own, parts) = lax.optimization_barrier((input_grad, (hidden, pieces)))
            cols_partner = to_partner(cols_of(parts, 1 - parity))
            cols_own = cols_of(parts, parity)
            pair = lax.dot_general(
                h_own, cols_own, (((0,), (0,)), ((), ())), preferred_element_type=jnp.float32
            ) + lax.dot_general(
                hidden_partner, cols_partner, (((0,), (0,)), ((), ())),
                preferred_element_type=jnp.float32,
            )
            own_g = me // 2
            total = lax.dynamic_slice_in_dim(pair, own_g * kv_block, kv_block, axis=1)
            outs = []
            for d in range(1, groups):
                dest_g = (own_g + d) % groups
                out = lax.dynamic_slice_in_dim(pair, dest_g * kv_block, kv_block, axis=1)
                outs.append(out.astype(jnp.bfloat16))
            for d, out in enumerate(outs, start=1):
                total = total + shifted(out, "dp", 2 * d).astype(jnp.float32)
            weight_total = total.astype(jnp.bfloat16)
        if c + 1 < CHUNKS:
            _, block = lax.optimization_barrier(((input_grad, outs), pieces[c + 1]))

    upstream = jnp.concatenate(inputs_grad, axis=0)
    pair_gain = gain_part + to_partner(gain_part)
    own_g = me // 2
    stacked = jnp.zeros((groups, d_local), jnp.float32)
    stacked = lax.dynamic_update_slice_in_dim(stacked, pair_gain[None], own_g, axis=0)
    for d in range(1, groups):
        got = shifted(pair_gain, "dp", 2 * d)
        stacked = lax.dynamic_update_slice_in_dim(stacked, got[None], (own_g - d) % groups, axis=0)
    gain_total = jnp.sum(stacked, axis=0)
    return (upstream[None, None], weight_total[None], gain_total[None])


def solution(mesh):
    in_specs = (
        P("dp", "pipe", None, "tensor"),
        P("dp", "pipe", None, "tensor"),
        P("dp", "pipe", None, "tensor"),
        P("pipe", "tensor"),
        P("pipe", "tensor", None),
    )
    out_specs = (P("dp", "pipe", None, "tensor"), P("pipe", "tensor", "dp"), P("pipe", "tensor"))
    return jax.shard_map(
        on_device, mesh=mesh, in_specs=in_specs, out_specs=out_specs, check_vma=False
    )
```

```python
import jax
import jax.numpy as jnp
from jax import lax
from jax.sharding import PartitionSpec as P

EPS = 1e-05
CHUNKS = 1


def from_behind(block, axis, distance):
    devices = range(lax.axis_size(axis))
    route = [(i - distance, i) for i in devices if i - distance in devices]
    return lax.ppermute(block, axis, route)


def shifted(block, axis, shift):
    n = lax.axis_size(axis)
    return lax.ppermute(block, axis, [(i, (i + shift) % n) for i in range(n)])


def to_partner(block):
    n = lax.axis_size("dp")
    return lax.ppermute(block, "dp", [(i, i ^ 1) for i in range(n)])


def on_device(layer_input, output_grad, kv_grad, norm_gain, kv_weight):
    rows = layer_input[0, 0]
    grad_out = output_grad[0, 0]
    grad_kv = kv_grad[0, 0]
    gain_f = norm_gain[0].astype(jnp.float32)
    weight = kv_weight[0]
    seq, d_local = rows.shape
    d_model = d_local * lax.axis_size("tensor")
    n_dp = lax.axis_size("dp")
    me = lax.axis_index("dp")
    parity = me % 2
    kv_block = grad_kv.shape[1] * lax.axis_size("tensor") // n_dp
    groups = n_dp // 2

    values = rows.astype(jnp.float32)
    total_squares = lax.psum(jnp.sum(values * values, axis=1, keepdims=True), "tensor")
    rstd = lax.rsqrt(total_squares / d_model + EPS)
    normed = values * rstd
    hidden = (normed * gain_f).astype(jnp.bfloat16)
    hidden_partner = to_partner(hidden)

    piece = lax.all_gather(grad_kv, "tensor", axis=1, tiled=True)

    def cols_of(p):
        return jnp.concatenate(
            [lax.dynamic_slice_in_dim(piece, (2 * g + p) * kv_block, kv_block, axis=1) for g in range(groups)],
            axis=1,
        )

    cols_partner = to_partner(cols_of(1 - parity))
    cols_own = cols_of(parity)

    step = seq // CHUNKS
    inputs_grad = []
    gain_part = jnp.zeros((d_local,), jnp.float32)
    block = piece[:step]
    weight_total = None
    for c in range(CHUNKS):
        lo = c * step
        row_total = lax.dot_general(
            block, weight, (((1,), (1,)), ((), ())), preferred_element_type=jnp.float32
        )
        normed_c = normed[lo:lo + step]
        scaled = gain_f * row_total
        mean_term = lax.psum(jnp.sum(scaled * normed_c, axis=1, keepdims=True), "tensor") / d_model
        input_grad = (
            grad_out[lo:lo + step].astype(jnp.float32)
            + rstd[lo:lo + step] * (scaled - normed_c * mean_term)
        ).astype(jnp.bfloat16)
        inputs_grad.append(from_behind(input_grad, "pipe", -1))
        gain_part = gain_part + jnp.sum(row_total * normed_c, axis=0)
        if c == 0:
            _, h_own = lax.optimization_barrier((input_grad, hidden))
            pair = lax.dot_general(
                h_own, cols_own, (((0,), (0,)), ((), ())), preferred_element_type=jnp.float32
            ) + lax.dot_general(
                hidden_partner, cols_partner, (((0,), (0,)), ((), ())),
                preferred_element_type=jnp.float32,
            )
            own_g = me // 2
            total = lax.dynamic_slice_in_dim(pair, own_g * kv_block, kv_block, axis=1)
            outs = []
            for d in range(1, groups):
                dest_g = (own_g + d) % groups
                out = lax.dynamic_slice_in_dim(pair, dest_g * kv_block, kv_block, axis=1)
                outs.append(out.astype(jnp.bfloat16))
            for d, out in enumerate(outs, start=1):
                total = total + shifted(out, "dp", 2 * d).astype(jnp.float32)
            weight_total = total.astype(jnp.bfloat16)
        if c + 1 < CHUNKS:
            _, block = lax.optimization_barrier(((input_grad, outs), piece[lo + step:lo + 2 * step]))

    upstream = jnp.concatenate(inputs_grad, axis=0)
    pair_gain = gain_part + to_partner(gain_part)
    own_g = me // 2
    stacked = jnp.zeros((groups, d_local), jnp.float32)
    stacked = lax.dynamic_update_slice_in_dim(stacked, pair_gain[None], own_g, axis=0)
    for d in range(1, groups):
        got = shifted(pair_gain, "dp", 2 * d)
        stacked = lax.dynamic_update_slice_in_dim(stacked, got[None], (own_g - d) % groups, axis=0)
    gain_total = jnp.sum(stacked, axis=0)
    return (upstream[None, None], weight_total[None], gain_total[None])


def solution(mesh):
    in_specs = (
        P("dp", "pipe", None, "tensor"),
        P("dp", "pipe", None, "tensor"),
        P("dp", "pipe", None, "tensor"),
        P("pipe", "tensor"),
        P("pipe", "tensor", None),
    )
    out_specs = (P("dp", "pipe", None, "tensor"), P("pipe", "tensor", "dp"), P("pipe", "tensor"))
    return jax.shard_map(
        on_device, mesh=mesh, in_specs=in_specs, out_specs=out_specs, check_vma=False
    )
```

```python
import jax
import jax.numpy as jnp
from jax import lax
from jax.sharding import PartitionSpec as P

D = 8192


def from_behind(block, axis, distance):
    devices = range(lax.axis_size(axis))
    route = [(i - distance, i) for i in devices if i - distance in devices]
    return lax.ppermute(block, axis, route)


def line_gather(block, axis):
    n = lax.axis_size(axis)
    me = lax.axis_index(axis)
    rows, width = block.shape
    right = [(i, i + 1) for i in range(n - 1)]
    left = [(i + 1, i) for i in range(n - 1)]
    full = jnp.zeros((rows, (3 * n - 2) * width), block.dtype)
    full = lax.dynamic_update_slice(full, block, (0, (me + n - 1) * width))
    from_left, from_right = block, block
    for k in range(1, n):
        from_left = lax.ppermute(from_left, axis, right)
        from_right = lax.ppermute(from_right, axis, left)
        full = lax.dynamic_update_slice(full, from_left, (0, (me - k + n - 1) * width))
        full = lax.dynamic_update_slice(full, from_right, (0, (me + k + n - 1) * width))
    return full[:, (n - 1) * width:(2 * n - 1) * width]


def on_device(layer_input, output_grad, kv_grad, norm_gain, kv_weight):
    rows = layer_input[0, 0]
    grad_out = output_grad[0, 0]
    grad_kv = kv_grad[0, 0]
    gain_f = norm_gain[0].astype(jnp.float32)
    weight = kv_weight[0]
    values = rows.astype(jnp.float32)
    local_squares = jnp.sum(values * values, axis=1, keepdims=True)
    total_squares = lax.psum(local_squares, "tensor")
    rstd = lax.rsqrt(total_squares / D + 1e-05)
    normed = values * rstd
    hidden = (normed * gain_f).astype(jnp.bfloat16)
    piece = line_gather(grad_kv, "tensor")
    row_total = lax.dot_general(
        piece, weight, (((1,), (1,)), ((), ())), preferred_element_type=jnp.float32
    )
    term = lax.dot_general(
        hidden, piece, (((0,), (0,)), ((), ())), preferred_element_type=jnp.float32
    )
    weight_total = term
    wgrad = weight_total
    scaled = gain_f * row_total
    local_dot = jnp.sum(scaled * normed, axis=1, keepdims=True)
    mean_term = lax.psum(local_dot, "tensor") / D
    input_grad = (grad_out.astype(jnp.float32) + rstd * (scaled - normed * mean_term)).astype(
        jnp.bfloat16
    )
    upstream = from_behind(input_grad, "pipe", -1)
    gain_part = jnp.sum(row_total * normed, axis=0)
    gain_total = lax.psum(gain_part, "dp")
    weight_total = lax.psum_scatter(
        wgrad.astype(jnp.bfloat16), "dp", scatter_dimension=1, tiled=True
    )
    return (upstream[None, None], weight_total[None], gain_total[None])


def solution(mesh):
    in_specs = (
        P("dp", "pipe", None, "tensor"),
        P("dp", "pipe", None, "tensor"),
        P("dp", "pipe", None, "tensor"),
        P("pipe", "tensor"),
        P("pipe", "tensor", None),
    )
    out_specs = (P("dp", "pipe", None, "tensor"), P("pipe", "tensor", "dp"), P("pipe", "tensor"))
    return jax.shard_map(
        on_device, mesh=mesh, in_specs=in_specs, out_specs=out_specs, check_vma=False
    )
```

```python
import jax
import jax.numpy as jnp
from jax import lax
from jax.sharding import PartitionSpec as P

EPS = 1e-05
CHUNKS = 2


def from_behind(block, axis, distance):
    devices = range(lax.axis_size(axis))
    route = [(i - distance, i) for i in devices if i - distance in devices]
    return lax.ppermute(block, axis, route)


def shifted(block, axis, shift):
    n = lax.axis_size(axis)
    return lax.ppermute(block, axis, [(i, (i + shift) % n) for i in range(n)])


def to_partner(block):
    n = lax.axis_size("dp")
    return lax.ppermute(block, "dp", [(i, i ^ 1) for i in range(n)])


def on_device(layer_input, output_grad, kv_grad, norm_gain, kv_weight):
    rows = layer_input[0, 0]
    grad_out = output_grad[0, 0]
    grad_kv = kv_grad[0, 0]
    gain_f = norm_gain[0].astype(jnp.float32)
    weight = kv_weight[0]
    seq, d_local = rows.shape
    d_model = d_local * lax.axis_size("tensor")
    n_dp = lax.axis_size("dp")
    me = lax.axis_index("dp")
    parity = me % 2
    kv_block = grad_kv.shape[1] * lax.axis_size("tensor") // n_dp
    groups = n_dp // 2

    values = rows.astype(jnp.float32)
    total_squares = lax.psum(jnp.sum(values * values, axis=1, keepdims=True), "tensor")
    rstd = lax.rsqrt(total_squares / d_model + EPS)
    normed = values * rstd
    hidden = (normed * gain_f).astype(jnp.bfloat16)
    hidden_partner = to_partner(hidden)

    step = seq // CHUNKS
    pieces = [
        lax.all_gather(grad_kv[c * step:(c + 1) * step], "tensor", axis=1, tiled=True)
        for c in range(CHUNKS)
    ]

    def cols_of(parts, p):
        return jnp.concatenate(
            [
                jnp.concatenate(
                    [lax.dynamic_slice_in_dim(q, (2 * g + p) * kv_block, kv_block, axis=1) for g in range(groups)],
                    axis=1,
                )
                for q in parts
            ],
            axis=0,
        )


    inputs_grad = []
    gain_part = jnp.zeros((d_local,), jnp.float32)
    block = pieces[0]
    weight_total = None
    for c in range(CHUNKS):
        lo = c * step
        row_total = lax.dot_general(
            block, weight, (((1,), (1,)), ((), ())), preferred_element_type=jnp.float32
        )
        normed_c = normed[lo:lo + step]
        scaled = gain_f * row_total
        mean_term = lax.psum(jnp.sum(scaled * normed_c, axis=1, keepdims=True), "tensor") / d_model
        input_grad = (
            grad_out[lo:lo + step].astype(jnp.float32)
            + rstd[lo:lo + step] * (scaled - normed_c * mean_term)
        ).astype(jnp.bfloat16)
        inputs_grad.append(from_behind(input_grad, "pipe", -1))
        gain_part = gain_part + jnp.sum(row_total * normed_c, axis=0)
        if c == 0:
            _, (h_own, parts) = lax.optimization_barrier((input_grad, (hidden, pieces)))
            cols_partner = to_partner(cols_of(parts, 1 - parity))
            cols_own = cols_of(parts, parity)
            pair = lax.dot_general(
                h_own, cols_own, (((0,), (0,)), ((), ())), preferred_element_type=jnp.float32
            ) + lax.dot_general(
                hidden_partner, cols_partner, (((0,), (0,)), ((), ())),
                preferred_element_type=jnp.float32,
            )
            own_g = me // 2
            total = lax.dynamic_slice_in_dim(pair, own_g * kv_block, kv_block, axis=1)
            outs = []
            for d in range(1, groups):
                dest_g = (own_g + d) % groups
                out = lax.dynamic_slice_in_dim(pair, dest_g * kv_block, kv_block, axis=1)
                outs.append(out.astype(jnp.bfloat16))
            for d, out in enumerate(outs, start=1):
                total = total + shifted(out, "dp", 2 * d).astype(jnp.float32)
            weight_total = total.astype(jnp.bfloat16)
        if c + 1 < CHUNKS:
            _, block = lax.optimization_barrier(((input_grad, outs), pieces[c + 1]))

    upstream = jnp.concatenate(inputs_grad, axis=0)
    pair_gain = gain_part + to_partner(gain_part)
    own_g = me // 2
    stacked = jnp.zeros((groups, d_local), jnp.float32)
    stacked = lax.dynamic_update_slice_in_dim(stacked, pair_gain[None], own_g, axis=0)
    for d in range(1, groups):
        got = shifted(pair_gain, "dp", 2 * d)
        stacked = lax.dynamic_update_slice_in_dim(stacked, got[None], (own_g - d) % groups, axis=0)
    gain_total = jnp.sum(stacked, axis=0)
    return (upstream[None, None], weight_total[None], gain_total[None])


def solution(mesh):
    in_specs = (
        P("dp", "pipe", None, "tensor"),
        P("dp", "pipe", None, "tensor"),
        P("dp", "pipe", None, "tensor"),
        P("pipe", "tensor"),
        P("pipe", "tensor", None),
    )
    out_specs = (P("dp", "pipe", None, "tensor"), P("pipe", "tensor", "dp"), P("pipe", "tensor"))
    return jax.shard_map(
        on_device, mesh=mesh, in_specs=in_specs, out_specs=out_specs, check_vma=False
    )
```

```python
import jax
import jax.numpy as jnp
from jax import lax
from jax.sharding import PartitionSpec as P

EPS = 1e-05
CHUNKS = 2


def from_behind(block, axis, distance):
    devices = range(lax.axis_size(axis))
    route = [(i - distance, i) for i in devices if i - distance in devices]
    return lax.ppermute(block, axis, route)


def shifted(block, axis, shift):
    n = lax.axis_size(axis)
    return lax.ppermute(block, axis, [(i, (i + shift) % n) for i in range(n)])


def to_partner(block):
    n = lax.axis_size("dp")
    return lax.ppermute(block, "dp", [(i, i ^ 1) for i in range(n)])


def on_device(layer_input, output_grad, kv_grad, norm_gain, kv_weight):
    rows = layer_input[0, 0]
    grad_out = output_grad[0, 0]
    grad_kv = kv_grad[0, 0]
    gain_f = norm_gain[0].astype(jnp.float32)
    weight = kv_weight[0]
    seq, d_local = rows.shape
    d_model = d_local * lax.axis_size("tensor")
    n_dp = lax.axis_size("dp")
    me = lax.axis_index("dp")
    parity = me % 2
    kv_block = grad_kv.shape[1] * lax.axis_size("tensor") // n_dp
    groups = n_dp // 2

    values = rows.astype(jnp.float32)
    total_squares = lax.psum(jnp.sum(values * values, axis=1, keepdims=True), "tensor")
    rstd = lax.rsqrt(total_squares / d_model + EPS)
    normed = values * rstd
    hidden = (normed * gain_f).astype(jnp.bfloat16)
    hidden_partner = to_partner(hidden)

    step = seq // CHUNKS
    pieces = [
        lax.all_gather(grad_kv[c * step:(c + 1) * step], "tensor", axis=1, tiled=True)
        for c in range(CHUNKS)
    ]

    def cols_of(parts, p):
        return jnp.concatenate(
            [
                jnp.concatenate(
                    [lax.dynamic_slice_in_dim(q, (2 * g + p) * kv_block, kv_block, axis=1) for g in range(groups)],
                    axis=1,
                )
                for q in parts
            ],
            axis=0,
        )


    inputs_grad = []
    gain_part = jnp.zeros((d_local,), jnp.float32)
    block = pieces[0]
    weight_total = None
    for c in range(CHUNKS):
        lo = c * step
        row_total = lax.dot_general(
            block, weight, (((1,), (1,)), ((), ())), preferred_element_type=jnp.float32
        )
        normed_c = normed[lo:lo + step]
        scaled = gain_f * row_total
        mean_term = lax.psum(jnp.sum(scaled * normed_c, axis=1, keepdims=True), "tensor") / d_model
        input_grad = (
            grad_out[lo:lo + step].astype(jnp.float32)
            + rstd[lo:lo + step] * (scaled - normed_c * mean_term)
        ).astype(jnp.bfloat16)
        inputs_grad.append(from_behind(input_grad, "pipe", -1))
        gain_part = gain_part + jnp.sum(row_total * normed_c, axis=0)
        if c == 0:
            _, (h_own, parts) = lax.optimization_barrier((input_grad, (hidden, pieces)))
            cols_partner = to_partner(cols_of(parts, 1 - parity))
            cols_own = cols_of(parts, parity)
            own_g = me // 2

            def pair_block(g):
                own_cols = lax.dynamic_slice_in_dim(cols_own, g * kv_block, kv_block, axis=1)
                partner_cols = lax.dynamic_slice_in_dim(cols_partner, g * kv_block, kv_block, axis=1)
                return lax.dot_general(
                    h_own, own_cols, (((0,), (0,)), ((), ())), preferred_element_type=jnp.float32
                ) + lax.dot_general(
                    hidden_partner, partner_cols, (((0,), (0,)), ((), ())),
                    preferred_element_type=jnp.float32,
                )

            outs = [pair_block((own_g + d) % groups).astype(jnp.bfloat16) for d in range(1, groups)]
            received = [shifted(out, "dp", 2 * d) for d, out in enumerate(outs, start=1)]
            _, h_own = lax.optimization_barrier((outs, h_own))
            total = pair_block(own_g)
            for got in received:
                total = total + got.astype(jnp.float32)
            weight_total = total.astype(jnp.bfloat16)
        if c + 1 < CHUNKS:
            _, block = lax.optimization_barrier(((input_grad, outs), pieces[c + 1]))

    upstream = jnp.concatenate(inputs_grad, axis=0)
    pair_gain = gain_part + to_partner(gain_part)
    own_g = me // 2
    stacked = jnp.zeros((groups, d_local), jnp.float32)
    stacked = lax.dynamic_update_slice_in_dim(stacked, pair_gain[None], own_g, axis=0)
    for d in range(1, groups):
        got = shifted(pair_gain, "dp", 2 * d)
        stacked = lax.dynamic_update_slice_in_dim(stacked, got[None], (own_g - d) % groups, axis=0)
    gain_total = jnp.sum(stacked, axis=0)
    return (upstream[None, None], weight_total[None], gain_total[None])


def solution(mesh):
    in_specs = (
        P("dp", "pipe", None, "tensor"),
        P("dp", "pipe", None, "tensor"),
        P("dp", "pipe", None, "tensor"),
        P("pipe", "tensor"),
        P("pipe", "tensor", None),
    )
    out_specs = (P("dp", "pipe", None, "tensor"), P("pipe", "tensor", "dp"), P("pipe", "tensor"))
    return jax.shard_map(
        on_device, mesh=mesh, in_specs=in_specs, out_specs=out_specs, check_vma=False
    )
```

```python
import jax
import jax.numpy as jnp
from jax import lax
from jax.sharding import PartitionSpec as P

EPS = 1e-05
CHUNKS = 2


def from_behind(block, axis, distance):
    devices = range(lax.axis_size(axis))
    route = [(i - distance, i) for i in devices if i - distance in devices]
    return lax.ppermute(block, axis, route)


def shifted(block, axis, shift):
    n = lax.axis_size(axis)
    return lax.ppermute(block, axis, [(i, (i + shift) % n) for i in range(n)])


def to_partner(block):
    n = lax.axis_size("dp")
    return lax.ppermute(block, "dp", [(i, i ^ 1) for i in range(n)])


def on_device(layer_input, output_grad, kv_grad, norm_gain, kv_weight):
    rows = layer_input[0, 0]
    grad_out = output_grad[0, 0]
    grad_kv = kv_grad[0, 0]
    gain_f = norm_gain[0].astype(jnp.float32)
    weight = kv_weight[0]
    seq, d_local = rows.shape
    d_model = d_local * lax.axis_size("tensor")
    n_dp = lax.axis_size("dp")
    me = lax.axis_index("dp")
    parity = me % 2
    kv_block = grad_kv.shape[1] * lax.axis_size("tensor") // n_dp
    groups = n_dp // 2

    values = rows.astype(jnp.float32)
    total_squares = lax.psum(jnp.sum(values * values, axis=1, keepdims=True), "tensor")
    rstd = lax.rsqrt(total_squares / d_model + EPS)
    normed = values * rstd
    hidden = (normed * gain_f).astype(jnp.bfloat16)
    hidden_partner = to_partner(hidden)

    step = seq // CHUNKS
    pieces = [
        lax.all_gather(grad_kv[c * step:(c + 1) * step], "tensor", axis=1, tiled=True)
        for c in range(CHUNKS)
    ]

    def cols_of(q, p):
        return jnp.concatenate(
            [lax.dynamic_slice_in_dim(q, (2 * g + p) * kv_block, kv_block, axis=1) for g in range(groups)],
            axis=1,
        )

    def tn(a, b):
        return lax.dot_general(a, b, (((0,), (0,)), ((), ())), preferred_element_type=jnp.float32)

    own_g = me // 2
    dests = [(own_g + d) % groups for d in range(1, groups)]

    def pair_blocks(h_own, h_partner, q):
        own_cols = cols_of(q, parity)
        partner_cols = to_partner(cols_of(q, 1 - parity))

        def block_of(g):
            oc = lax.dynamic_slice_in_dim(own_cols, g * kv_block, kv_block, axis=1)
            pc = lax.dynamic_slice_in_dim(partner_cols, g * kv_block, kv_block, axis=1)
            return tn(h_own, oc) + tn(h_partner, pc)

        return block_of

    inputs_grad = []
    gain_part = jnp.zeros((d_local,), jnp.float32)
    block = pieces[0]
    weight_total = None
    for c in range(CHUNKS):
        lo = c * step
        row_total = lax.dot_general(
            block, weight, (((1,), (1,)), ((), ())), preferred_element_type=jnp.float32
        )
        normed_c = normed[lo:lo + step]
        scaled = gain_f * row_total
        mean_term = lax.psum(jnp.sum(scaled * normed_c, axis=1, keepdims=True), "tensor") / d_model
        input_grad = (
            grad_out[lo:lo + step].astype(jnp.float32)
            + rstd[lo:lo + step] * (scaled - normed_c * mean_term)
        ).astype(jnp.bfloat16)
        inputs_grad.append(from_behind(input_grad, "pipe", -1))
        gain_part = gain_part + jnp.sum(row_total * normed_c, axis=0)
        if c == 0:
            _, (h, hp, parts) = lax.optimization_barrier((input_grad, (hidden, hidden_partner, pieces)))
            chunk_blocks = [
                pair_blocks(h[k * step:(k + 1) * step], hp[k * step:(k + 1) * step], parts[k])
                for k in range(CHUNKS)
            ]
            outs = []
            for g in dests:
                acc = chunk_blocks[0](g)
                for k in range(1, CHUNKS):
                    acc = acc + chunk_blocks[k](g)
                outs.append(acc.astype(jnp.bfloat16))
            received = [shifted(out, "dp", 2 * d) for d, out in enumerate(outs, start=1)]
            _, first = lax.optimization_barrier((outs, chunk_blocks[0](own_g)))
            total = first
            for k in range(1, CHUNKS):
                total = total + chunk_blocks[k](own_g)
            for got in received:
                total = total + got.astype(jnp.float32)
            weight_total = total.astype(jnp.bfloat16)
        if c + 1 < CHUNKS:
            _, block = lax.optimization_barrier(((input_grad, outs), parts[c + 1]))

    upstream = jnp.concatenate(inputs_grad, axis=0)
    pair_gain = gain_part + to_partner(gain_part)
    own_g = me // 2
    stacked = jnp.zeros((groups, d_local), jnp.float32)
    stacked = lax.dynamic_update_slice_in_dim(stacked, pair_gain[None], own_g, axis=0)
    for d in range(1, groups):
        got = shifted(pair_gain, "dp", 2 * d)
        stacked = lax.dynamic_update_slice_in_dim(stacked, got[None], (own_g - d) % groups, axis=0)
    gain_total = jnp.sum(stacked, axis=0)
    return (upstream[None, None], weight_total[None], gain_total[None])


def solution(mesh):
    in_specs = (
        P("dp", "pipe", None, "tensor"),
        P("dp", "pipe", None, "tensor"),
        P("dp", "pipe", None, "tensor"),
        P("pipe", "tensor"),
        P("pipe", "tensor", None),
    )
    out_specs = (P("dp", "pipe", None, "tensor"), P("pipe", "tensor", "dp"), P("pipe", "tensor"))
    return jax.shard_map(
        on_device, mesh=mesh, in_specs=in_specs, out_specs=out_specs, check_vma=False
    )
```

```python
import jax
import jax.numpy as jnp
from jax import lax
from jax.sharding import PartitionSpec as P

EPS = 1e-05
CHUNKS = 2


def from_behind(block, axis, distance):
    devices = range(lax.axis_size(axis))
    route = [(i - distance, i) for i in devices if i - distance in devices]
    return lax.ppermute(block, axis, route)


def shifted(block, axis, shift):
    n = lax.axis_size(axis)
    return lax.ppermute(block, axis, [(i, (i + shift) % n) for i in range(n)])


def to_partner(block):
    n = lax.axis_size("dp")
    return lax.ppermute(block, "dp", [(i, i ^ 1) for i in range(n)])


def on_device(layer_input, output_grad, kv_grad, norm_gain, kv_weight):
    rows = layer_input[0, 0]
    grad_out = output_grad[0, 0]
    grad_kv = kv_grad[0, 0]
    gain_f = norm_gain[0].astype(jnp.float32)
    weight = kv_weight[0]
    seq, d_local = rows.shape
    d_model = d_local * lax.axis_size("tensor")
    n_dp = lax.axis_size("dp")
    me = lax.axis_index("dp")
    parity = me % 2
    kv_block = grad_kv.shape[1] * lax.axis_size("tensor") // n_dp
    groups = n_dp // 2

    values = rows.astype(jnp.float32)
    total_squares = lax.psum(jnp.sum(values * values, axis=1, keepdims=True), "tensor")
    rstd = lax.rsqrt(total_squares / d_model + EPS)
    normed = values * rstd
    hidden = (normed * gain_f).astype(jnp.bfloat16)
    hidden_partner = to_partner(hidden)

    step = seq // CHUNKS
    pieces = [
        lax.all_gather(grad_kv[c * step:(c + 1) * step], "tensor", axis=1, tiled=True)
        for c in range(CHUNKS)
    ]

    def cols_of(q, p):
        return jnp.concatenate(
            [lax.dynamic_slice_in_dim(q, (2 * g + p) * kv_block, kv_block, axis=1) for g in range(groups)],
            axis=1,
        )

    def tn(a, b):
        return lax.dot_general(a, b, (((0,), (0,)), ((), ())), preferred_element_type=jnp.float32)

    own_g = me // 2
    dests = [(own_g + d) % groups for d in range(1, groups)]

    def pair_blocks(h_own, h_partner, q):
        own_cols = cols_of(q, parity)
        partner_cols = to_partner(cols_of(q, 1 - parity))

        def block_of(g, rows):
            oc = lax.dynamic_slice_in_dim(own_cols, g * kv_block, kv_block, axis=1)
            pc = lax.dynamic_slice_in_dim(partner_cols, g * kv_block, kv_block, axis=1)
            return tn(h_own[:, rows], oc) + tn(h_partner[:, rows], pc)

        return block_of

    inputs_grad = []
    gain_part = jnp.zeros((d_local,), jnp.float32)
    block = pieces[0]
    weight_total = None
    for c in range(CHUNKS):
        lo = c * step
        row_total = lax.dot_general(
            block, weight, (((1,), (1,)), ((), ())), preferred_element_type=jnp.float32
        )
        normed_c = normed[lo:lo + step]
        scaled = gain_f * row_total
        mean_term = lax.psum(jnp.sum(scaled * normed_c, axis=1, keepdims=True), "tensor") / d_model
        input_grad = (
            grad_out[lo:lo + step].astype(jnp.float32)
            + rstd[lo:lo + step] * (scaled - normed_c * mean_term)
        ).astype(jnp.bfloat16)
        inputs_grad.append(from_behind(input_grad, "pipe", -1))
        gain_part = gain_part + jnp.sum(row_total * normed_c, axis=0)
        if c == 0:
            _, (h, hp, parts) = lax.optimization_barrier((input_grad, (hidden, hidden_partner, pieces)))
            chunk_blocks = [
                pair_blocks(h[k * step:(k + 1) * step], hp[k * step:(k + 1) * step], parts[k])
                for k in range(CHUNKS)
            ]
            halves = [slice(0, d_local // 2), slice(d_local // 2, d_local)]
            outs, received = [], []
            for rows_half in halves:
                for d, g in enumerate(dests, start=1):
                    acc = chunk_blocks[0](g, rows_half)
                    for k in range(1, CHUNKS):
                        acc = acc + chunk_blocks[k](g, rows_half)
                    out = acc.astype(jnp.bfloat16)
                    outs.append(out)
                    received.append(shifted(out, "dp", 2 * d))
            _, h_first = lax.optimization_barrier((outs, [chunk_blocks[0](own_g, r) for r in halves]))
            pieces_out = []
            n_dest = len(dests)
            for i_half, rows_half in enumerate(halves):
                total = h_first[i_half]
                for k in range(1, CHUNKS):
                    total = total + chunk_blocks[k](own_g, rows_half)
                for got in received[i_half * n_dest:(i_half + 1) * n_dest]:
                    total = total + got.astype(jnp.float32)
                pieces_out.append(total.astype(jnp.bfloat16))
            total = jnp.concatenate(pieces_out, axis=0)
            weight_total = total
        if c + 1 < CHUNKS:
            _, block = lax.optimization_barrier(((input_grad, outs), parts[c + 1]))

    upstream = jnp.concatenate(inputs_grad, axis=0)
    pair_gain = gain_part + to_partner(gain_part)
    own_g = me // 2
    stacked = jnp.zeros((groups, d_local), jnp.float32)
    stacked = lax.dynamic_update_slice_in_dim(stacked, pair_gain[None], own_g, axis=0)
    for d in range(1, groups):
        got = shifted(pair_gain, "dp", 2 * d)
        stacked = lax.dynamic_update_slice_in_dim(stacked, got[None], (own_g - d) % groups, axis=0)
    gain_total = jnp.sum(stacked, axis=0)
    return (upstream[None, None], weight_total[None], gain_total[None])


def solution(mesh):
    in_specs = (
        P("dp", "pipe", None, "tensor"),
        P("dp", "pipe", None, "tensor"),
        P("dp", "pipe", None, "tensor"),
        P("pipe", "tensor"),
        P("pipe", "tensor", None),
    )
    out_specs = (P("dp", "pipe", None, "tensor"), P("pipe", "tensor", "dp"), P("pipe", "tensor"))
    return jax.shard_map(
        on_device, mesh=mesh, in_specs=in_specs, out_specs=out_specs, check_vma=False
    )
```

```python
import jax
import jax.numpy as jnp
from jax import lax
from jax.sharding import PartitionSpec as P

EPS = 1e-05
CHUNKS = 2


def from_behind(block, axis, distance):
    devices = range(lax.axis_size(axis))
    route = [(i - distance, i) for i in devices if i - distance in devices]
    return lax.ppermute(block, axis, route)


def shifted(block, axis, shift):
    n = lax.axis_size(axis)
    return lax.ppermute(block, axis, [(i, (i + shift) % n) for i in range(n)])


def to_partner(block):
    n = lax.axis_size("dp")
    return lax.ppermute(block, "dp", [(i, i ^ 1) for i in range(n)])


def gather_columns(block):
    n = lax.axis_size("tensor")
    me = lax.axis_index("tensor")
    rows, width = block.shape
    full = jnp.zeros((rows, width * n), block.dtype)
    full = lax.dynamic_update_slice(full, block, (0, me * width))
    for d in range(1, n):
        got = shifted(block, "tensor", d)
        full = lax.dynamic_update_slice(full, got, (0, ((me - d) % n) * width))
    return full


def on_device(layer_input, output_grad, kv_grad, norm_gain, kv_weight):
    rows = layer_input[0, 0]
    grad_out = output_grad[0, 0]
    grad_kv = kv_grad[0, 0]
    gain_f = norm_gain[0].astype(jnp.float32)
    weight = kv_weight[0]
    seq, d_local = rows.shape
    d_model = d_local * lax.axis_size("tensor")
    n_dp = lax.axis_size("dp")
    me = lax.axis_index("dp")
    parity = me % 2
    kv_block = grad_kv.shape[1] * lax.axis_size("tensor") // n_dp
    groups = n_dp // 2

    values = rows.astype(jnp.float32)
    total_squares = lax.psum(jnp.sum(values * values, axis=1, keepdims=True), "tensor")
    rstd = lax.rsqrt(total_squares / d_model + EPS)
    normed = values * rstd
    hidden = (normed * gain_f).astype(jnp.bfloat16)
    hidden_partner = to_partner(hidden)

    step = seq // CHUNKS
    pieces = [lax.all_gather(grad_kv[:step], "tensor", axis=1, tiled=True)] + [
        gather_columns(grad_kv[c * step:(c + 1) * step]) for c in range(1, CHUNKS)
    ]

    def cols_of(q, p):
        return jnp.concatenate(
            [lax.dynamic_slice_in_dim(q, (2 * g + p) * kv_block, kv_block, axis=1) for g in range(groups)],
            axis=1,
        )

    def tn(a, b):
        return lax.dot_general(a, b, (((0,), (0,)), ((), ())), preferred_element_type=jnp.float32)

    own_g = me // 2
    dests = [(own_g + d) % groups for d in range(1, groups)]

    def pair_blocks(h_own, h_partner, q):
        own_cols = cols_of(q, parity)
        partner_cols = to_partner(cols_of(q, 1 - parity))

        def block_of(g):
            oc = lax.dynamic_slice_in_dim(own_cols, g * kv_block, kv_block, axis=1)
            pc = lax.dynamic_slice_in_dim(partner_cols, g * kv_block, kv_block, axis=1)
            return tn(h_own, oc) + tn(h_partner, pc)

        return block_of

    inputs_grad = []
    gain_part = jnp.zeros((d_local,), jnp.float32)
    block = pieces[0]
    weight_total = None
    for c in range(CHUNKS):
        lo = c * step
        row_total = lax.dot_general(
            block, weight, (((1,), (1,)), ((), ())), preferred_element_type=jnp.float32
        )
        normed_c = normed[lo:lo + step]
        scaled = gain_f * row_total
        mean_term = lax.psum(jnp.sum(scaled * normed_c, axis=1, keepdims=True), "tensor") / d_model
        input_grad = (
            grad_out[lo:lo + step].astype(jnp.float32)
            + rstd[lo:lo + step] * (scaled - normed_c * mean_term)
        ).astype(jnp.bfloat16)
        inputs_grad.append(from_behind(input_grad, "pipe", -1))
        gain_part = gain_part + jnp.sum(row_total * normed_c, axis=0)
        if c == 0:
            _, (h, hp, parts) = lax.optimization_barrier((input_grad, (hidden, hidden_partner, pieces)))
            chunk_blocks = [
                pair_blocks(h[k * step:(k + 1) * step], hp[k * step:(k + 1) * step], parts[k])
                for k in range(CHUNKS)
            ]
            outs = []
            for g in dests:
                acc = chunk_blocks[0](g)
                for k in range(1, CHUNKS):
                    acc = acc + chunk_blocks[k](g)
                outs.append(acc.astype(jnp.bfloat16))
            received = [shifted(out, "dp", 2 * d) for d, out in enumerate(outs, start=1)]
            _, first = lax.optimization_barrier((outs, chunk_blocks[0](own_g)))
            total = first
            for k in range(1, CHUNKS):
                total = total + chunk_blocks[k](own_g)
            for got in received:
                total = total + got.astype(jnp.float32)
            weight_total = total.astype(jnp.bfloat16)
        if c + 1 < CHUNKS:
            _, block = lax.optimization_barrier(((input_grad, outs), parts[c + 1]))

    upstream = jnp.concatenate(inputs_grad, axis=0)
    pair_gain = gain_part + to_partner(gain_part)
    own_g = me // 2
    stacked = jnp.zeros((groups, d_local), jnp.float32)
    stacked = lax.dynamic_update_slice_in_dim(stacked, pair_gain[None], own_g, axis=0)
    for d in range(1, groups):
        got = shifted(pair_gain, "dp", 2 * d)
        stacked = lax.dynamic_update_slice_in_dim(stacked, got[None], (own_g - d) % groups, axis=0)
    gain_total = jnp.sum(stacked, axis=0)
    return (upstream[None, None], weight_total[None], gain_total[None])


def solution(mesh):
    in_specs = (
        P("dp", "pipe", None, "tensor"),
        P("dp", "pipe", None, "tensor"),
        P("dp", "pipe", None, "tensor"),
        P("pipe", "tensor"),
        P("pipe", "tensor", None),
    )
    out_specs = (P("dp", "pipe", None, "tensor"), P("pipe", "tensor", "dp"), P("pipe", "tensor"))
    return jax.shard_map(
        on_device, mesh=mesh, in_specs=in_specs, out_specs=out_specs, check_vma=False
    )
```

```python
import jax
import jax.numpy as jnp
from jax import lax
from jax.sharding import PartitionSpec as P

EPS = 1e-05
CHUNKS = 2


def from_behind(block, axis, distance):
    devices = range(lax.axis_size(axis))
    route = [(i - distance, i) for i in devices if i - distance in devices]
    return lax.ppermute(block, axis, route)


def shifted(block, axis, shift):
    n = lax.axis_size(axis)
    return lax.ppermute(block, axis, [(i, (i + shift) % n) for i in range(n)])


def to_partner(block):
    n = lax.axis_size("dp")
    return lax.ppermute(block, "dp", [(i, i ^ 1) for i in range(n)])


def on_device(layer_input, output_grad, kv_grad, norm_gain, kv_weight):
    rows = layer_input[0, 0]
    grad_out = output_grad[0, 0]
    grad_kv = kv_grad[0, 0]
    gain_f = norm_gain[0].astype(jnp.float32)
    weight = kv_weight[0]
    seq, d_local = rows.shape
    d_model = d_local * lax.axis_size("tensor")
    n_dp = lax.axis_size("dp")
    me = lax.axis_index("dp")
    parity = me % 2
    kv_block = grad_kv.shape[1] * lax.axis_size("tensor") // n_dp
    groups = n_dp // 2

    values = rows.astype(jnp.float32)
    total_squares = lax.psum(jnp.sum(values * values, axis=1, keepdims=True), "tensor")
    rstd = lax.rsqrt(total_squares / d_model + EPS)
    normed = values * rstd
    hidden = (normed * gain_f).astype(jnp.bfloat16)
    hidden_partner = to_partner(hidden)

    step = seq // CHUNKS
    pieces = [
        lax.all_gather(grad_kv[c * step:(c + 1) * step], "tensor", axis=1, tiled=True)
        for c in range(CHUNKS)
    ]

    def cols_of(q, p):
        return jnp.concatenate(
            [lax.dynamic_slice_in_dim(q, (2 * g + p) * kv_block, kv_block, axis=1) for g in range(groups)],
            axis=1,
        )

    def tn(a, b):
        return lax.dot_general(a, b, (((0,), (0,)), ((), ())), preferred_element_type=jnp.float32)

    own_g = me // 2
    dests = [(own_g + d) % groups for d in range(1, groups)]

    def pair_blocks(h_own, h_partner, own_cols, partner_cols):
        def block_of(g):
            oc = lax.dynamic_slice_in_dim(own_cols, g * kv_block, kv_block, axis=1)
            pc = lax.dynamic_slice_in_dim(partner_cols, g * kv_block, kv_block, axis=1)
            return tn(h_own, oc) + tn(h_partner, pc)

        return block_of

    inputs_grad = []
    gain_part = jnp.zeros((d_local,), jnp.float32)
    block = pieces[0]
    weight_total = None
    for c in range(CHUNKS):
        lo = c * step
        row_total = lax.dot_general(
            block, weight, (((1,), (1,)), ((), ())), preferred_element_type=jnp.float32
        )
        normed_c = normed[lo:lo + step]
        scaled = gain_f * row_total
        mean_term = lax.psum(jnp.sum(scaled * normed_c, axis=1, keepdims=True), "tensor") / d_model
        input_grad = (
            grad_out[lo:lo + step].astype(jnp.float32)
            + rstd[lo:lo + step] * (scaled - normed_c * mean_term)
        ).astype(jnp.bfloat16)
        inputs_grad.append(from_behind(input_grad, "pipe", -1))
        gain_part = gain_part + jnp.sum(row_total * normed_c, axis=0)
        if c == 0:
            _, (h, hp, parts) = lax.optimization_barrier((input_grad, (hidden, hidden_partner, pieces)))
            chunk_inputs = [
                (
                    h[k * step:(k + 1) * step],
                    hp[k * step:(k + 1) * step],
                    cols_of(parts[k], parity),
                    to_partner(cols_of(parts[k], 1 - parity)),
                )
                for k in range(CHUNKS)
            ]
            chunk_blocks = [pair_blocks(*inputs) for inputs in chunk_inputs]
            outs = []
            for g in dests:
                acc = chunk_blocks[0](g)
                for k in range(1, CHUNKS):
                    acc = acc + chunk_blocks[k](g)
                outs.append(acc.astype(jnp.bfloat16))
            received = [shifted(out, "dp", 2 * d) for d, out in enumerate(outs, start=1)]
            _, later_inputs = lax.optimization_barrier((outs, chunk_inputs))
            later_blocks = [pair_blocks(*inputs) for inputs in later_inputs]
            total = later_blocks[0](own_g)
            for k in range(1, CHUNKS):
                total = total + later_blocks[k](own_g)
            for got in received:
                total = total + got.astype(jnp.float32)
            weight_total = total.astype(jnp.bfloat16)
        if c + 1 < CHUNKS:
            _, block = lax.optimization_barrier(((input_grad, outs), parts[c + 1]))

    upstream = jnp.concatenate(inputs_grad, axis=0)
    pair_gain = gain_part + to_partner(gain_part)
    own_g = me // 2
    stacked = jnp.zeros((groups, d_local), jnp.float32)
    stacked = lax.dynamic_update_slice_in_dim(stacked, pair_gain[None], own_g, axis=0)
    for d in range(1, groups):
        got = shifted(pair_gain, "dp", 2 * d)
        stacked = lax.dynamic_update_slice_in_dim(stacked, got[None], (own_g - d) % groups, axis=0)
    gain_total = jnp.sum(stacked, axis=0)
    return (upstream[None, None], weight_total[None], gain_total[None])


def solution(mesh):
    in_specs = (
        P("dp", "pipe", None, "tensor"),
        P("dp", "pipe", None, "tensor"),
        P("dp", "pipe", None, "tensor"),
        P("pipe", "tensor"),
        P("pipe", "tensor", None),
    )
    out_specs = (P("dp", "pipe", None, "tensor"), P("pipe", "tensor", "dp"), P("pipe", "tensor"))
    return jax.shard_map(
        on_device, mesh=mesh, in_specs=in_specs, out_specs=out_specs, check_vma=False
    )
```

```python
import jax
import jax.numpy as jnp
from jax import lax
from jax.sharding import PartitionSpec as P

EPS = 1e-05
CHUNKS = 2


def from_behind(block, axis, distance):
    devices = range(lax.axis_size(axis))
    route = [(i - distance, i) for i in devices if i - distance in devices]
    return lax.ppermute(block, axis, route)


def shifted(block, axis, shift):
    n = lax.axis_size(axis)
    return lax.ppermute(block, axis, [(i, (i + shift) % n) for i in range(n)])


def to_partner(block):
    n = lax.axis_size("dp")
    return lax.ppermute(block, "dp", [(i, i ^ 1) for i in range(n)])


def on_device(layer_input, output_grad, kv_grad, norm_gain, kv_weight):
    rows = layer_input[0, 0]
    grad_out = output_grad[0, 0]
    grad_kv = kv_grad[0, 0]
    gain_f = norm_gain[0].astype(jnp.float32)
    weight = kv_weight[0]
    seq, d_local = rows.shape
    d_model = d_local * lax.axis_size("tensor")
    n_dp = lax.axis_size("dp")
    me = lax.axis_index("dp")
    parity = me % 2
    kv_block = grad_kv.shape[1] * lax.axis_size("tensor") // n_dp
    groups = n_dp // 2

    values = rows.astype(jnp.float32)
    total_squares = lax.psum(jnp.sum(values * values, axis=1, keepdims=True), "tensor")
    rstd = lax.rsqrt(total_squares / d_model + EPS)
    normed = values * rstd
    hidden = (normed * gain_f).astype(jnp.bfloat16)
    hidden_partner = to_partner(hidden)

    step = seq // CHUNKS
    pieces = [
        lax.all_gather(grad_kv[c * step:(c + 1) * step], "tensor", axis=1, tiled=True)
        for c in range(CHUNKS)
    ]

    def cols_of(q, p):
        return jnp.concatenate(
            [lax.dynamic_slice_in_dim(q, (2 * g + p) * kv_block, kv_block, axis=1) for g in range(groups)],
            axis=1,
        )

    def tn(a, b):
        return lax.dot_general(a, b, (((0,), (0,)), ((), ())), preferred_element_type=jnp.float32)

    own_g = me // 2
    dests = [(own_g + d) % groups for d in range(1, groups)]

    def pair_blocks(h_own, h_partner, q):
        own_cols = cols_of(q, parity)
        partner_cols = to_partner(cols_of(q, 1 - parity))

        def block_of(g):
            oc = lax.dynamic_slice_in_dim(own_cols, g * kv_block, kv_block, axis=1)
            pc = lax.dynamic_slice_in_dim(partner_cols, g * kv_block, kv_block, axis=1)
            return tn(h_own, oc) + tn(h_partner, pc)

        return block_of

    inputs_grad = []
    gain_part = jnp.zeros((d_local,), jnp.float32)
    block = pieces[0]
    weight_total = None
    for c in range(CHUNKS):
        lo = c * step
        row_total = lax.dot_general(
            block, weight, (((1,), (1,)), ((), ())), preferred_element_type=jnp.float32
        )
        normed_c = normed[lo:lo + step]
        scaled = gain_f * row_total
        mean_term = lax.psum(jnp.sum(scaled * normed_c, axis=1, keepdims=True), "tensor") / d_model
        input_grad = (
            grad_out[lo:lo + step].astype(jnp.float32)
            + rstd[lo:lo + step] * (scaled - normed_c * mean_term)
        ).astype(jnp.bfloat16)
        inputs_grad.append(from_behind(input_grad, "pipe", -1))
        gain_part = gain_part + jnp.sum(row_total * normed_c, axis=0)
        if c == 0:
            _, (h, hp, first_part) = lax.optimization_barrier((input_grad, (hidden, hidden_partner, pieces[0])))
            first_blocks = pair_blocks(h[:step], hp[:step], first_part)
            first_sends = [first_blocks(g) for g in dests]
            _, later = lax.optimization_barrier((first_sends, pieces[1:]))
            parts = [first_part] + list(later)
            chunk_blocks = [first_blocks] + [
                pair_blocks(h[k * step:(k + 1) * step], hp[k * step:(k + 1) * step], parts[k])
                for k in range(1, CHUNKS)
            ]
            outs = []
            for i, g in enumerate(dests):
                acc = first_sends[i]
                for k in range(1, CHUNKS):
                    acc = acc + chunk_blocks[k](g)
                outs.append(acc.astype(jnp.bfloat16))
            received = [shifted(out, "dp", 2 * d) for d, out in enumerate(outs, start=1)]
            _, first = lax.optimization_barrier((outs, chunk_blocks[0](own_g)))
            total = first
            for k in range(1, CHUNKS):
                total = total + chunk_blocks[k](own_g)
            for got in received:
                total = total + got.astype(jnp.float32)
            weight_total = total.astype(jnp.bfloat16)
        if c + 1 < CHUNKS:
            _, block = lax.optimization_barrier(((input_grad, outs), parts[c + 1]))

    upstream = jnp.concatenate(inputs_grad, axis=0)
    pair_gain = gain_part + to_partner(gain_part)
    own_g = me // 2
    stacked = jnp.zeros((groups, d_local), jnp.float32)
    stacked = lax.dynamic_update_slice_in_dim(stacked, pair_gain[None], own_g, axis=0)
    for d in range(1, groups):
        got = shifted(pair_gain, "dp", 2 * d)
        stacked = lax.dynamic_update_slice_in_dim(stacked, got[None], (own_g - d) % groups, axis=0)
    gain_total = jnp.sum(stacked, axis=0)
    return (upstream[None, None], weight_total[None], gain_total[None])


def solution(mesh):
    in_specs = (
        P("dp", "pipe", None, "tensor"),
        P("dp", "pipe", None, "tensor"),
        P("dp", "pipe", None, "tensor"),
        P("pipe", "tensor"),
        P("pipe", "tensor", None),
    )
    out_specs = (P("dp", "pipe", None, "tensor"), P("pipe", "tensor", "dp"), P("pipe", "tensor"))
    return jax.shard_map(
        on_device, mesh=mesh, in_specs=in_specs, out_specs=out_specs, check_vma=False
    )
```

```python
import jax
import jax.numpy as jnp
from jax import lax
from jax.sharding import PartitionSpec as P

EPS = 1e-05
CHUNKS = 2


def from_behind(block, axis, distance):
    devices = range(lax.axis_size(axis))
    route = [(i - distance, i) for i in devices if i - distance in devices]
    return lax.ppermute(block, axis, route)


def shifted(block, axis, shift):
    n = lax.axis_size(axis)
    return lax.ppermute(block, axis, [(i, (i + shift) % n) for i in range(n)])


def to_partner(block):
    n = lax.axis_size("dp")
    return lax.ppermute(block, "dp", [(i, i ^ 1) for i in range(n)])


def on_device(layer_input, output_grad, kv_grad, norm_gain, kv_weight):
    rows = layer_input[0, 0]
    grad_out = output_grad[0, 0]
    grad_kv = kv_grad[0, 0]
    gain_f = norm_gain[0].astype(jnp.float32)
    weight = kv_weight[0]
    seq, d_local = rows.shape
    d_model = d_local * lax.axis_size("tensor")
    n_dp = lax.axis_size("dp")
    me = lax.axis_index("dp")
    parity = me % 2
    kv_block = grad_kv.shape[1] * lax.axis_size("tensor") // n_dp
    groups = n_dp // 2

    values = rows.astype(jnp.float32)
    total_squares = lax.psum(jnp.sum(values * values, axis=1, keepdims=True), "tensor")
    rstd = lax.rsqrt(total_squares / d_model + EPS)
    normed = values * rstd
    hidden = (normed * gain_f).astype(jnp.bfloat16)
    hidden_partner = to_partner(hidden)

    step = seq // CHUNKS
    pieces = [
        lax.all_gather(grad_kv[c * step:(c + 1) * step], "tensor", axis=1, tiled=True)
        for c in range(CHUNKS)
    ]

    def cols_of(q, p):
        return jnp.concatenate(
            [lax.dynamic_slice_in_dim(q, (2 * g + p) * kv_block, kv_block, axis=1) for g in range(groups)],
            axis=1,
        )

    def tn(a, b):
        return lax.dot_general(a, b, (((0,), (0,)), ((), ())), preferred_element_type=jnp.float32)

    own_g = me // 2
    dests = [(own_g + d) % groups for d in range(1, groups)]

    def pair_blocks(h_own, h_partner, q):
        own_cols = cols_of(q, parity)
        partner_cols = to_partner(cols_of(q, 1 - parity))

        def block_of(g):
            oc = lax.dynamic_slice_in_dim(own_cols, g * kv_block, kv_block, axis=1)
            pc = lax.dynamic_slice_in_dim(partner_cols, g * kv_block, kv_block, axis=1)
            return tn(h_own, oc) + tn(h_partner, pc)

        return block_of

    inputs_grad = []
    gain_part = jnp.zeros((d_local,), jnp.float32)
    block = pieces[0]
    weight_total = None
    for c in range(CHUNKS):
        lo = c * step
        row_total = lax.dot_general(
            block, weight, (((1,), (1,)), ((), ())), preferred_element_type=jnp.float32
        )
        normed_c = normed[lo:lo + step]
        scaled = gain_f * row_total
        mean_term = lax.psum(jnp.sum(scaled * normed_c, axis=1, keepdims=True), "tensor") / d_model
        input_grad = (
            grad_out[lo:lo + step].astype(jnp.float32)
            + rstd[lo:lo + step] * (scaled - normed_c * mean_term)
        ).astype(jnp.bfloat16)
        inputs_grad.append(from_behind(input_grad, "pipe", -1))
        gain_part = gain_part + jnp.sum(row_total * normed_c, axis=0)
        if c == 0:
            _, (h, hp, parts) = lax.optimization_barrier((input_grad, (hidden, hidden_partner, pieces)))
            chunk_blocks = [
                pair_blocks(h[k * step:(k + 1) * step], hp[k * step:(k + 1) * step], parts[k])
                for k in range(CHUNKS)
            ]
            outs = []
            for g in dests:
                acc = chunk_blocks[0](g)
                for k in range(1, CHUNKS):
                    acc = acc + chunk_blocks[k](g)
                outs.append(acc.astype(jnp.bfloat16))
            received = [shifted(out, "dp", 2 * d) for d, out in enumerate(outs, start=1)]
            _, first = lax.optimization_barrier((outs, chunk_blocks[0](own_g)))
            total = first
            for k in range(1, CHUNKS):
                total = total + chunk_blocks[k](own_g)
            total = lax.optimization_barrier(total)
            for got in received:
                total = total + got.astype(jnp.float32)
            weight_total = total.astype(jnp.bfloat16)
        if c + 1 < CHUNKS:
            _, block = lax.optimization_barrier(((input_grad, outs), parts[c + 1]))

    upstream = jnp.concatenate(inputs_grad, axis=0)
    pair_gain = gain_part + to_partner(gain_part)
    own_g = me // 2
    stacked = jnp.zeros((groups, d_local), jnp.float32)
    stacked = lax.dynamic_update_slice_in_dim(stacked, pair_gain[None], own_g, axis=0)
    for d in range(1, groups):
        got = shifted(pair_gain, "dp", 2 * d)
        stacked = lax.dynamic_update_slice_in_dim(stacked, got[None], (own_g - d) % groups, axis=0)
    gain_total = jnp.sum(stacked, axis=0)
    return (upstream[None, None], weight_total[None], gain_total[None])


def solution(mesh):
    in_specs = (
        P("dp", "pipe", None, "tensor"),
        P("dp", "pipe", None, "tensor"),
        P("dp", "pipe", None, "tensor"),
        P("pipe", "tensor"),
        P("pipe", "tensor", None),
    )
    out_specs = (P("dp", "pipe", None, "tensor"), P("pipe", "tensor", "dp"), P("pipe", "tensor"))
    return jax.shard_map(
        on_device, mesh=mesh, in_specs=in_specs, out_specs=out_specs, check_vma=False
    )
```

```python
import jax
import jax.numpy as jnp
from jax import lax
from jax.sharding import PartitionSpec as P

EPS = 1e-05
CHUNKS = 2


def from_behind(block, axis, distance):
    devices = range(lax.axis_size(axis))
    route = [(i - distance, i) for i in devices if i - distance in devices]
    return lax.ppermute(block, axis, route)


def shifted(block, axis, shift):
    n = lax.axis_size(axis)
    return lax.ppermute(block, axis, [(i, (i + shift) % n) for i in range(n)])


def to_partner(block):
    n = lax.axis_size("dp")
    return lax.ppermute(block, "dp", [(i, i ^ 1) for i in range(n)])


def on_device(layer_input, output_grad, kv_grad, norm_gain, kv_weight):
    rows = layer_input[0, 0]
    grad_out = output_grad[0, 0]
    grad_kv = kv_grad[0, 0]
    gain_f = norm_gain[0].astype(jnp.float32)
    weight = kv_weight[0]
    seq, d_local = rows.shape
    d_model = d_local * lax.axis_size("tensor")
    n_dp = lax.axis_size("dp")
    me = lax.axis_index("dp")
    parity = me % 2
    kv_block = grad_kv.shape[1] * lax.axis_size("tensor") // n_dp
    groups = n_dp // 2

    values = rows.astype(jnp.float32)
    total_squares = lax.psum(jnp.sum(values * values, axis=1, keepdims=True), "tensor")
    rstd = lax.rsqrt(total_squares / d_model + EPS)
    normed = values * rstd
    hidden = (normed * gain_f).astype(jnp.bfloat16)
    hidden_partner = to_partner(hidden)

    step = seq // CHUNKS
    pieces = [
        lax.all_gather(grad_kv[c * step:(c + 1) * step], "tensor", axis=1, tiled=True)
        for c in range(CHUNKS)
    ]

    def cols_of(q, p):
        return jnp.concatenate(
            [lax.dynamic_slice_in_dim(q, (2 * g + p) * kv_block, kv_block, axis=1) for g in range(groups)],
            axis=1,
        )

    def tn(a, b):
        return lax.dot_general(a, b, (((0,), (0,)), ((), ())), preferred_element_type=jnp.float32)

    own_g = me // 2
    dests = [(own_g + d) % groups for d in range(1, groups)]

    def pair_blocks(h_own, h_partner, q):
        own_cols = cols_of(q, parity)
        partner_cols = to_partner(cols_of(q, 1 - parity))

        def block_of(g):
            oc = lax.dynamic_slice_in_dim(own_cols, g * kv_block, kv_block, axis=1)
            pc = lax.dynamic_slice_in_dim(partner_cols, g * kv_block, kv_block, axis=1)
            return tn(h_own, oc) + tn(h_partner, pc)

        return block_of

    inputs_grad = []
    gain_part = jnp.zeros((d_local,), jnp.float32)
    block = pieces[0]
    weight_total = None
    for c in range(CHUNKS):
        lo = c * step
        row_total = lax.dot_general(
            block, weight, (((1,), (1,)), ((), ())), preferred_element_type=jnp.float32
        )
        normed_c = normed[lo:lo + step]
        scaled = gain_f * row_total
        mean_term = lax.psum(jnp.sum(scaled * normed_c, axis=1, keepdims=True), "tensor") / d_model
        input_grad = (
            grad_out[lo:lo + step].astype(jnp.float32)
            + rstd[lo:lo + step] * (scaled - normed_c * mean_term)
        ).astype(jnp.bfloat16)
        inputs_grad.append(from_behind(input_grad, "pipe", -1))
        gain_part = gain_part + jnp.sum(row_total * normed_c, axis=0)
        if c == 0:
            _, (h, hp, parts) = lax.optimization_barrier((input_grad, (hidden, hidden_partner, pieces)))
            chunk_blocks = [
                pair_blocks(h[k * step:(k + 1) * step], hp[k * step:(k + 1) * step], parts[k])
                for k in range(CHUNKS)
            ]
            outs = []
            for g in dests:
                acc = chunk_blocks[0](g)
                for k in range(1, CHUNKS):
                    acc = acc + chunk_blocks[k](g)
                outs.append(acc.astype(jnp.bfloat16))
            received = [shifted(out, "dp", 2 * d) for d, out in enumerate(outs, start=1)]
            _, first = lax.optimization_barrier((outs, chunk_blocks[0](own_g)))
            total = first
            for k in range(1, CHUNKS):
                total = total + chunk_blocks[k](own_g)
            total = lax.optimization_barrier(total)
            for got in received:
                total = total + got.astype(jnp.float32)
            weight_total = total.astype(jnp.bfloat16)
        if c + 1 < CHUNKS:
            _, block = lax.optimization_barrier(((input_grad, outs), parts[c + 1]))

    upstream = jnp.concatenate(inputs_grad, axis=0)
    pair_gain = gain_part + to_partner(gain_part)
    upstream, pair_gain = lax.optimization_barrier((upstream, pair_gain))
    own_g = me // 2
    stacked = jnp.zeros((groups, d_local), jnp.float32)
    stacked = lax.dynamic_update_slice_in_dim(stacked, pair_gain[None], own_g, axis=0)
    for d in range(1, groups):
        got = shifted(pair_gain, "dp", 2 * d)
        stacked = lax.dynamic_update_slice_in_dim(stacked, got[None], (own_g - d) % groups, axis=0)
    gain_total = jnp.sum(stacked, axis=0)
    return (upstream[None, None], weight_total[None], gain_total[None])


def solution(mesh):
    in_specs = (
        P("dp", "pipe", None, "tensor"),
        P("dp", "pipe", None, "tensor"),
        P("dp", "pipe", None, "tensor"),
        P("pipe", "tensor"),
        P("pipe", "tensor", None),
    )
    out_specs = (P("dp", "pipe", None, "tensor"), P("pipe", "tensor", "dp"), P("pipe", "tensor"))
    return jax.shard_map(
        on_device, mesh=mesh, in_specs=in_specs, out_specs=out_specs, check_vma=False
    )
```

```python
import jax
import jax.numpy as jnp
from jax import lax
from jax.sharding import PartitionSpec as P

EPS = 1e-05
CHUNKS = 2


def from_behind(block, axis, distance):
    devices = range(lax.axis_size(axis))
    route = [(i - distance, i) for i in devices if i - distance in devices]
    return lax.ppermute(block, axis, route)


def shifted(block, axis, shift):
    n = lax.axis_size(axis)
    return lax.ppermute(block, axis, [(i, (i + shift) % n) for i in range(n)])


def to_partner(block):
    n = lax.axis_size("dp")
    return lax.ppermute(block, "dp", [(i, i ^ 1) for i in range(n)])


def on_device(layer_input, output_grad, kv_grad, norm_gain, kv_weight):
    rows = layer_input[0, 0]
    grad_out = output_grad[0, 0]
    grad_kv = kv_grad[0, 0]
    gain_f = norm_gain[0].astype(jnp.float32)
    weight = kv_weight[0]
    seq, d_local = rows.shape
    d_model = d_local * lax.axis_size("tensor")
    n_dp = lax.axis_size("dp")
    me = lax.axis_index("dp")
    parity = me % 2
    kv_block = grad_kv.shape[1] * lax.axis_size("tensor") // n_dp
    groups = n_dp // 2

    values = rows.astype(jnp.float32)
    total_squares = lax.psum(jnp.sum(values * values, axis=1, keepdims=True), "tensor")
    rstd = lax.rsqrt(total_squares / d_model + EPS)
    normed = values * rstd
    hidden = (normed * gain_f).astype(jnp.bfloat16)
    hidden_partner = to_partner(hidden)

    step = seq // CHUNKS
    pieces = [
        lax.all_gather(grad_kv[c * step:(c + 1) * step], "tensor", axis=1, tiled=True)
        for c in range(CHUNKS)
    ]

    def cols_of(q, p):
        return jnp.concatenate(
            [lax.dynamic_slice_in_dim(q, (2 * g + p) * kv_block, kv_block, axis=1) for g in range(groups)],
            axis=1,
        )

    def tn(a, b):
        return lax.dot_general(a, b, (((0,), (0,)), ((), ())), preferred_element_type=jnp.float32)

    own_g = me // 2
    dests = [(own_g + d) % groups for d in range(1, groups)]

    def pair_blocks(h_own, h_partner, q):
        own_cols = cols_of(q, parity)
        partner_cols = to_partner(cols_of(q, 1 - parity))

        def block_of(g):
            oc = lax.dynamic_slice_in_dim(own_cols, g * kv_block, kv_block, axis=1)
            pc = lax.dynamic_slice_in_dim(partner_cols, g * kv_block, kv_block, axis=1)
            return tn(h_own, oc) + tn(h_partner, pc)

        return block_of

    inputs_grad = []
    gain_part = jnp.zeros((d_local,), jnp.float32)
    block = pieces[0]
    weight_total = None
    for c in range(CHUNKS):
        lo = c * step
        row_total = lax.dot_general(
            block, weight, (((1,), (1,)), ((), ())), preferred_element_type=jnp.float32
        )
        normed_c = normed[lo:lo + step]
        scaled = gain_f * row_total
        mean_term = lax.psum(jnp.sum(scaled * normed_c, axis=1, keepdims=True), "tensor") / d_model
        input_grad = (
            grad_out[lo:lo + step].astype(jnp.float32)
            + rstd[lo:lo + step] * (scaled - normed_c * mean_term)
        ).astype(jnp.bfloat16)
        inputs_grad.append(from_behind(input_grad, "pipe", -1))
        gain_part = gain_part + jnp.sum(row_total * normed_c, axis=0)
        if c == 0:
            _, (h, hp, parts) = lax.optimization_barrier((input_grad, (hidden, hidden_partner, pieces)))
            chunk_blocks = [
                pair_blocks(h[k * step:(k + 1) * step], hp[k * step:(k + 1) * step], parts[k])
                for k in range(CHUNKS)
            ]
            outs = []
            for g in dests:
                acc = chunk_blocks[0](g)
                for k in range(1, CHUNKS):
                    acc = acc + chunk_blocks[k](g)
                outs.append(acc.astype(jnp.bfloat16))
            received = [shifted(out, "dp", 2 * d) for d, out in enumerate(outs, start=1)]
            _, first = lax.optimization_barrier((outs, chunk_blocks[0](own_g)))
            total = first
            for k in range(1, CHUNKS):
                total = total + chunk_blocks[k](own_g)
            own_total = total
        if c + 1 < CHUNKS:
            _, block = lax.optimization_barrier(((input_grad, outs), parts[c + 1]))

    inputs_grad, own_total = lax.optimization_barrier((inputs_grad, own_total))
    upstream = jnp.concatenate(inputs_grad, axis=0)
    pair_gain = gain_part + to_partner(gain_part)
    upstream, pair_gain = lax.optimization_barrier((upstream, pair_gain))
    own_g = me // 2
    stacked = jnp.zeros((groups, d_local), jnp.float32)
    stacked = lax.dynamic_update_slice_in_dim(stacked, pair_gain[None], own_g, axis=0)
    for d in range(1, groups):
        got = shifted(pair_gain, "dp", 2 * d)
        stacked = lax.dynamic_update_slice_in_dim(stacked, got[None], (own_g - d) % groups, axis=0)
    gain_total = jnp.sum(stacked, axis=0)
    total = own_total
    for got in received:
        total = total + got.astype(jnp.float32)
    weight_total = total.astype(jnp.bfloat16)
    return (upstream[None, None], weight_total[None], gain_total[None])


def solution(mesh):
    in_specs = (
        P("dp", "pipe", None, "tensor"),
        P("dp", "pipe", None, "tensor"),
        P("dp", "pipe", None, "tensor"),
        P("pipe", "tensor"),
        P("pipe", "tensor", None),
    )
    out_specs = (P("dp", "pipe", None, "tensor"), P("pipe", "tensor", "dp"), P("pipe", "tensor"))
    return jax.shard_map(
        on_device, mesh=mesh, in_specs=in_specs, out_specs=out_specs, check_vma=False
    )
```

```python
import jax
import jax.numpy as jnp
from jax import lax
from jax.sharding import PartitionSpec as P

EPS = 1e-05
CHUNKS = 2


def from_behind(block, axis, distance):
    devices = range(lax.axis_size(axis))
    route = [(i - distance, i) for i in devices if i - distance in devices]
    return lax.ppermute(block, axis, route)


def shifted(block, axis, shift):
    n = lax.axis_size(axis)
    return lax.ppermute(block, axis, [(i, (i + shift) % n) for i in range(n)])


def to_partner(block):
    n = lax.axis_size("dp")
    return lax.ppermute(block, "dp", [(i, i ^ 1) for i in range(n)])


def on_device(layer_input, output_grad, kv_grad, norm_gain, kv_weight):
    rows = layer_input[0, 0]
    grad_out = output_grad[0, 0]
    grad_kv = kv_grad[0, 0]
    gain_f = norm_gain[0].astype(jnp.float32)
    weight = kv_weight[0]
    seq, d_local = rows.shape
    d_model = d_local * lax.axis_size("tensor")
    n_dp = lax.axis_size("dp")
    me = lax.axis_index("dp")
    parity = me % 2
    kv_block = grad_kv.shape[1] * lax.axis_size("tensor") // n_dp
    groups = n_dp // 2

    values = rows.astype(jnp.float32)
    total_squares = lax.psum(jnp.sum(values * values, axis=1, keepdims=True), "tensor")
    rstd = lax.rsqrt(total_squares / d_model + EPS)
    normed = values * rstd
    hidden = (normed * gain_f).astype(jnp.bfloat16)
    hidden_partner = to_partner(hidden)

    step = seq // CHUNKS
    pieces = [
        lax.all_gather(grad_kv[c * step:(c + 1) * step], "tensor", axis=1, tiled=True)
        for c in range(CHUNKS)
    ]

    def cols_of(q, p):
        return jnp.concatenate(
            [lax.dynamic_slice_in_dim(q, (2 * g + p) * kv_block, kv_block, axis=1) for g in range(groups)],
            axis=1,
        )

    def tn(a, b):
        return lax.dot_general(a, b, (((0,), (0,)), ((), ())), preferred_element_type=jnp.float32)

    own_g = me // 2
    dests = [(own_g + d) % groups for d in range(1, groups)]

    def pair_blocks(h_own, h_partner, q):
        own_cols = cols_of(q, parity)
        partner_cols = to_partner(cols_of(q, 1 - parity))

        def block_of(g):
            oc = lax.dynamic_slice_in_dim(own_cols, g * kv_block, kv_block, axis=1)
            pc = lax.dynamic_slice_in_dim(partner_cols, g * kv_block, kv_block, axis=1)
            return tn(h_own, oc) + tn(h_partner, pc)

        return block_of

    inputs_grad = []
    gain_part = jnp.zeros((d_local,), jnp.float32)
    block = pieces[0]
    weight_total = None
    for c in range(CHUNKS):
        lo = c * step
        row_total = lax.dot_general(
            block, weight, (((1,), (1,)), ((), ())), preferred_element_type=jnp.float32
        )
        normed_c = normed[lo:lo + step]
        scaled = gain_f * row_total
        mean_term = lax.psum(jnp.sum(scaled * normed_c, axis=1, keepdims=True), "tensor") / d_model
        input_grad = (
            grad_out[lo:lo + step].astype(jnp.float32)
            + rstd[lo:lo + step] * (scaled - normed_c * mean_term)
        ).astype(jnp.bfloat16)
        inputs_grad.append(from_behind(input_grad, "pipe", -1))
        gain_part = gain_part + jnp.sum(row_total * normed_c, axis=0)
        if c == 0:
            _, (h, hp, parts) = lax.optimization_barrier((input_grad, (hidden, hidden_partner, pieces)))
            chunk_blocks = [
                pair_blocks(h[k * step:(k + 1) * step], hp[k * step:(k + 1) * step], parts[k])
                for k in range(CHUNKS)
            ]
            outs = []
            for g in dests:
                acc = chunk_blocks[0](g)
                for k in range(1, CHUNKS):
                    acc = acc + chunk_blocks[k](g)
                outs.append(acc.astype(jnp.bfloat16))
            received = [shifted(out, "dp", 2 * d) for d, out in enumerate(outs, start=1)]
            _, first = lax.optimization_barrier((outs, chunk_blocks[0](own_g)))
            total = first
            for k in range(1, CHUNKS):
                total = total + chunk_blocks[k](own_g)
            total = lax.optimization_barrier(total.astype(jnp.bfloat16)).astype(jnp.float32)
            for got in received:
                total = total + got.astype(jnp.float32)
            weight_total = total.astype(jnp.bfloat16)
        if c + 1 < CHUNKS:
            _, block = lax.optimization_barrier(((input_grad, outs), parts[c + 1]))

    upstream = jnp.concatenate(inputs_grad, axis=0)
    pair_gain = gain_part + to_partner(gain_part)
    own_g = me // 2
    stacked = jnp.zeros((groups, d_local), jnp.float32)
    stacked = lax.dynamic_update_slice_in_dim(stacked, pair_gain[None], own_g, axis=0)
    for d in range(1, groups):
        got = shifted(pair_gain, "dp", 2 * d)
        stacked = lax.dynamic_update_slice_in_dim(stacked, got[None], (own_g - d) % groups, axis=0)
    gain_total = jnp.sum(stacked, axis=0)
    return (upstream[None, None], weight_total[None], gain_total[None])


def solution(mesh):
    in_specs = (
        P("dp", "pipe", None, "tensor"),
        P("dp", "pipe", None, "tensor"),
        P("dp", "pipe", None, "tensor"),
        P("pipe", "tensor"),
        P("pipe", "tensor", None),
    )
    out_specs = (P("dp", "pipe", None, "tensor"), P("pipe", "tensor", "dp"), P("pipe", "tensor"))
    return jax.shard_map(
        on_device, mesh=mesh, in_specs=in_specs, out_specs=out_specs, check_vma=False
    )
```
